1024 devices in a mesh: gx: 16 (over y, core), gy: 64 (over z, x).
Axes of the slice: x: 8, y: 8, z: 8, core: 2. Of those that a mesh axis runs over, the one named last changes fastest.
Arguments:
- positions: float32 [16, 64, 5, 3, 128], P('gx', 'gy'), may hold values from 0 to 80, as said below
- polarity: float32 [16, 64, 5, 128], P('gx', 'gy'), may hold values from 0.25 to 1.25
- direct_field: float32 [16, 64, 5, 6, 128], P('gx', 'gy'), may hold values from -30 to 30
- atom_count: int32 [16, 64, 5], P('gx', 'gy'), may hold values from 64 to 128, as said below
- pair_list: int32 [16, 64, 3, 61], P('gx', 'gy'), may hold values from 0 to 4, as said below
- pair_count: int32 [16, 64], P('gx', 'gy'), may hold values from 9 to 61, as said below
Outputs:
- dipoles: float32 [16, 64, 5, 6, 128], P('gx', 'gy')
- residual: float32 [16, 64, 5, 6, 128], P('gx', 'gy')
The draws below stay inside these ranges and needn't reach their ends.
Inputs may be any that keep to these rules, and one draw needn't show every extreme that they name: `positions`: coordinates lie in the device's column, the first two in [0, 8), the third in [0, 80); any two atoms, also of neighbouring columns placed as in the reference program, are at least 1 apart. `atom_count`: every device has one block with all 128 atoms. `pair_list`: for e < pair_count the entry (b, s, c) has s in 0..4; with s = 0, c is b or b + 1, otherwise c is b - 1, b or b + 1, all blocks within 0..4; no entry appears twice; every device lists all its s = 0 entries; entries from pair_count on are zeros. `pair_count`: some device lists all 61 possible entries.
All inputs are finite; a program needn't handle non-finite values.
Results may differ from the reference program's by a relative error of at most 0.003.
Values sent between devices are 32-bit elements; how exact they have to be, the bound alone decides.
No kernel may reach another device: no remote copies, remote signals or barrier semaphores. Data moves between devices by JAX's collectives and lax.ppermute only.
A program may use at most 32 MiB of HBM per device.

```python
import math
from functools import partial
import jax
import jax.numpy as jnp
from jax import lax

ATOMS = 128
BLOCKS = 5
ITERS = 2
PAIR_CAP = 61
SLAB_X = 16
SLAB_Y = 64


def draw_positions(key, part):
    full_shape = (SLAB_X, SLAB_Y, BLOCKS, 3, ATOMS)
    atom_index = jnp.arange(ATOMS)
    lattice_x = 2.0 * (atom_index % 4).astype(jnp.float32) + 1.0
    lattice_y = 2.0 * (atom_index // 4 % 4).astype(jnp.float32) + 1.0
    layer_z = 2.0 * (atom_index // 16).astype(jnp.float32) + 1.0
    block_base = (jnp.arange(BLOCKS) * (ATOMS // 8)).astype(jnp.float32)
    lattice_z = block_base[:, None] + layer_z[None, :]
    lattice = jnp.stack([jnp.broadcast_to(lattice_x[None, :], (BLOCKS, ATOMS)), jnp.broadcast_to(lattice_y[None, :], (BLOCKS, ATOMS)), lattice_z], axis=1)
    jitter = jax.random.uniform(key, full_shape, jnp.float32, -0.499, 0.499)
    return lattice[None, None] + jitter


def draw_direct_field(key, part):
    key_base, key_scale = jax.random.split(key)
    full_shape = (SLAB_X, SLAB_Y, BLOCKS, 6, ATOMS)
    fraction_x = jnp.arange(SLAB_X).astype(jnp.float32) / max(SLAB_X - 1, 1)
    fraction_y = jnp.arange(SLAB_Y).astype(jnp.float32) / max(SLAB_Y - 1, 1)
    rising = 1.0 + fraction_x[:, None] + fraction_y[None, :]
    base_noise = jnp.clip(jax.random.normal(key_base, full_shape, jnp.float32), -4.0, 4.0)
    atom_scale = jnp.exp(jax.random.uniform(key_scale, (SLAB_X, SLAB_Y, BLOCKS, 1, ATOMS), jnp.float32, math.log(0.3), math.log(3.0)))
    return 0.3 * base_noise * rising[:, :, None, None, None] * atom_scale


def draw_atom_count(key, part):
    key_count, key_full = jax.random.split(key)
    counts = jax.random.randint(key_count, (SLAB_X, SLAB_Y, BLOCKS), ATOMS // 2, ATOMS + 1)
    full_block = jax.random.randint(key_full, (SLAB_X, SLAB_Y, 1), 0, BLOCKS)
    block_id = jnp.arange(BLOCKS)[None, None, :]
    return jnp.where(block_id == full_block, ATOMS, counts).astype(jnp.int32)


def pair_tables(key):
    base_key = jax.random.fold_in(key, 7)
    key_keep, key_level, key_full, key_order = jax.random.split(base_key, 4)
    candidates = 15 * BLOCKS
    flat_index = jnp.arange(candidates)
    slot_id = flat_index // (3 * BLOCKS)
    block_id = flat_index // 3 % BLOCKS
    other_id = block_id + flat_index % 3 - 1
    valid_pair = (other_id >= 0) & (other_id < BLOCKS) & ((slot_id > 0) | (other_id >= block_id))
    density_level = jax.random.randint(key_level, (SLAB_X, SLAB_Y, 1), 4, 11)
    chance = density_level * density_level
    device_id = jnp.arange(SLAB_X * SLAB_Y).reshape(SLAB_X, SLAB_Y, 1)
    full_device = jax.random.randint(key_full, (), 0, SLAB_X * SLAB_Y)
    chance = jnp.where(device_id == full_device, 100, chance)
    roll_value = jax.random.randint(key_keep, (SLAB_X, SLAB_Y, candidates), 0, 100)
    keep_pair = valid_pair[None, None, :] & ((slot_id[None, None, :] == 0) | (roll_value < chance))
    order_score = jax.random.randint(key_order, (SLAB_X, SLAB_Y, candidates), 0, 65536) * candidates + flat_index[None, None, :]
    order_score = jnp.where(keep_pair, order_score, 65536 * candidates + order_score)
    order_index = jnp.argsort(order_score, axis=-1, stable=True)[:, :, :PAIR_CAP]
    pair_total = jnp.sum(keep_pair.astype(jnp.int32), axis=-1)
    table = jnp.stack([jnp.take(block_id, order_index), jnp.take(slot_id, order_index), jnp.take(other_id, order_index)], axis=2)
    live_rows = jnp.arange(PAIR_CAP)[None, None, None, :] < pair_total[:, :, None, None]
    table = jnp.where(live_rows, table, 0)
    return (table.astype(jnp.int32), pair_total.astype(jnp.int32))


def draw_pair_list(key, part):
    return pair_tables(key)[0]


def draw_pair_count(key, part):
    return pair_tables(key)[1]


def shard_levels(rng, shape, shards, smallest, high):
    gain, own = 1.0, jax.random.fold_in(rng, 6)
    for axis_at, parts in shards:
        heights = jnp.exp(jax.random.uniform(jax.random.fold_in(own, axis_at), (parts,), jnp.float32, smallest / len(shards), high / len(shards)))
        gain = gain * jnp.repeat(heights, shape[axis_at] // parts).reshape([-1 if axis == axis_at else 1 for axis in range(len(shape))])
    return gain


def setup_inputs(seed: int = 0) -> dict:
    seeds = jax.random.split(jax.random.key(seed), 7)
    return {
        "positions": draw_positions(jax.random.fold_in(seeds[6], 71), 0),
        "polarity": jnp.clip(jnp.exp(math.log(1.25) - 1.609438 * jax.random.uniform(seeds[1], (SLAB_X, SLAB_Y, BLOCKS, ATOMS), jnp.float32) ** shard_levels(seeds[1], (SLAB_X, SLAB_Y, BLOCKS, ATOMS), ((0, 16), (1, 64)), -0.2, 0.2)), 0.25, 1.25),
        "direct_field": draw_direct_field(jax.random.fold_in(seeds[6], 71), 0),
        "atom_count": draw_atom_count(jax.random.fold_in(seeds[6], 71), 0),
        "pair_list": draw_pair_list(jax.random.fold_in(seeds[6], 71), 0),
        "pair_count": draw_pair_count(jax.random.fold_in(seeds[6], 71), 0),
    }


thole_factor = 0.39
column_width = 8.0
pair_batch = 8
slot_shift_x = (0.0, 0.0, 1.0, 1.0, 1.0)
slot_shift_y = (0.0, 1.0, -1.0, 0.0, 1.0)
slot_moves = ((0, 0), (0, 1), (1, -1), (1, 0), (1, 1))

def tensor_apply(coef_three, coef_five, deltas, moment, axis_sum):
    if axis_sum == 2:
        moments = [moment[:, member, None, :] for member in range(3)]
    else:
        moments = [moment[:, member, :, None] for member in range(3)]
    project = deltas[0] * moments[0] + deltas[1] * moments[1] + deltas[2] * moments[2]
    scaled = coef_five * project
    return jnp.stack([lax.optimization_barrier(jnp.sum(scaled * deltas[member] - coef_three * moments[member], axis=axis_sum)) for member in range(3)], axis=1)

def pair_fields(geom_i, geom_j, dip_i, dip_j, slot_ids, same_block):
    chosen = (slot_ids[:, None] == jnp.arange(5, dtype=jnp.int32)[None, :]).astype(jnp.float32)
    offset_x = column_width * lax.optimization_barrier(jnp.sum(chosen * jnp.array(slot_shift_x, jnp.float32)[None, :], axis=1))
    offset_y = column_width * lax.optimization_barrier(jnp.sum(chosen * jnp.array(slot_shift_y, jnp.float32)[None, :], axis=1))
    delta_x = geom_j[:, 0, None, :] + offset_x[:, None, None] - geom_i[:, 0, :, None]
    delta_y = geom_j[:, 1, None, :] + offset_y[:, None, None] - geom_i[:, 1, :, None]
    delta_z = geom_j[:, 2, None, :] - geom_i[:, 2, :, None]
    dist_sq = delta_x * delta_x + delta_y * delta_y + delta_z * delta_z
    atom_width = geom_i.shape[2]
    same_atom = jnp.arange(atom_width)[:, None] == jnp.arange(atom_width)[None, :]
    diagonal = same_atom[None, :, :] & same_block[:, None, None]
    dist_sq = jnp.where(diagonal, 1.0, dist_sq)
    inv_dist = lax.rsqrt(dist_sq)
    inv_cube = inv_dist * inv_dist * inv_dist
    root_pol = jnp.sqrt(geom_i[:, 3, :, None] * geom_j[:, 3, None, :])
    damping = thole_factor * dist_sq * jnp.sqrt(dist_sq) / root_pol
    lambda_three = -jnp.expm1(-damping)
    lambda_five = lambda_three - damping * jnp.exp(-damping)
    keep_pair = jnp.where(diagonal, 0.0, 1.0)
    coef_three = keep_pair * lambda_three * inv_cube
    coef_five = keep_pair * 3.0 * lambda_five * inv_cube * inv_dist * inv_dist
    deltas = (delta_x, delta_y, delta_z)
    forward = jnp.concatenate([tensor_apply(coef_three, coef_five, deltas, dip_j[:, 0:3], 2), tensor_apply(coef_three, coef_five, deltas, dip_j[:, 3:6], 2)], axis=1)
    backward = jnp.concatenate([tensor_apply(coef_three, coef_five, deltas, dip_i[:, 0:3], 1), tensor_apply(coef_three, coef_five, deltas, dip_i[:, 3:6], 1)], axis=1)
    return (forward, backward)

def accumulate(geom_stack, dip_stack, entries, pair_total, live_turns, capacity_turns):
    blocks = geom_stack.shape[0] // 5
    atom_width = geom_stack.shape[2]
    targets = jnp.arange(5 * blocks, dtype=jnp.int32)
    padded = jnp.pad(entries, ((0, 0), (0, capacity_turns * pair_batch - entries.shape[1])))

    def one_turn(turn_index, accumulated):
        first_row = (turn_index * pair_batch).astype(jnp.int32)
        group_rows = lax.dynamic_slice_in_dim(padded, first_row, pair_batch, 1)
        own_block = group_rows[0]
        slot_ids = group_rows[1]
        other_block = group_rows[2]
        source = slot_ids * blocks + other_block
        live_rows = (first_row + jnp.arange(pair_batch, dtype=jnp.int32) < pair_total).astype(jnp.float32)
        same_block = (slot_ids == 0) & (own_block == other_block)
        forward, backward = pair_fields(jnp.take(geom_stack, own_block, axis=0), jnp.take(geom_stack, source, axis=0), jnp.take(dip_stack, own_block, axis=0), jnp.take(dip_stack, source, axis=0), slot_ids, same_block)
        to_own = (own_block[:, None] == targets[None, :]).astype(jnp.float32) * live_rows[:, None]
        twoway = live_rows * (1.0 - same_block.astype(jnp.float32))
        to_other = (source[:, None] == targets[None, :]).astype(jnp.float32) * twoway[:, None]
        accumulated = accumulated + jnp.einsum('gt,gca->tca', to_own, forward, precision=lax.Precision.HIGHEST)
        return accumulated + jnp.einsum('gt,gca->tca', to_other, backward, precision=lax.Precision.HIGHEST)
    return lax.fori_loop(0, live_turns, one_turn, jnp.zeros((5 * blocks, 6, atom_width), jnp.float32))

def neighbour_stack(whole_array):
    slot_arrays = [jnp.roll(whole_array, (-moves[0], -moves[1]), axis=(0, 1)) for moves in slot_moves]
    return jnp.stack(slot_arrays, axis=2)

def set_sums(first_vec, second_vec):
    product = (first_vec * second_vec).reshape(SLAB_X, SLAB_Y, BLOCKS, 2, 3, ATOMS)
    return lax.optimization_barrier(jnp.sum(product, axis=(0, 1, 2, 4, 5)))

def spread_sets(values):
    return jnp.repeat(values, 3)[:, None]

def reference(positions, polarity, direct_field, atom_count, pair_list, pair_count):
    atom_mask = (jnp.arange(ATOMS, dtype=jnp.int32)[None, None, None, :] < atom_count[:, :, :, None]).astype(jnp.float32)
    pol_wide = polarity[:, :, :, None, :]
    geometry = jnp.concatenate([positions, pol_wide], axis=3)
    geom_stack = neighbour_stack(geometry).reshape(SLAB_X, SLAB_Y, 5 * BLOCKS, 4, ATOMS)
    capacity_turns = -(-PAIR_CAP // pair_batch)
    per_device = jax.vmap(partial(accumulate, live_turns=capacity_turns, capacity_turns=capacity_turns))

    def one_row(row_data):
        return per_device(row_data[0], row_data[1], row_data[2], row_data[3])

    def operate(search):
        dip_stack = neighbour_stack(search).reshape(SLAB_X, SLAB_Y, 5 * BLOCKS, 6, ATOMS)
        accumulated = lax.map(one_row, (geom_stack, dip_stack, pair_list, pair_count))
        accumulated = accumulated.reshape(SLAB_X, SLAB_Y, 5, BLOCKS, 6, ATOMS)
        own_total = accumulated[:, :, 0]
        for slot_index in range(1, 5):
            own_total = own_total + jnp.roll(accumulated[:, :, slot_index], slot_moves[slot_index], axis=(0, 1))
        return search / pol_wide - own_total * atom_mask[:, :, :, None, :]
    residual = direct_field * atom_mask[:, :, :, None, :]
    dipoles = jnp.zeros_like(residual)
    search = pol_wide * residual
    rho_now = set_sums(residual, search)
    for iteration in range(ITERS):
        image_vec = operate(search)
        step_size = spread_sets(rho_now / set_sums(search, image_vec))
        dipoles = dipoles + step_size * search
        residual = residual - step_size * image_vec
        if iteration + 1 < ITERS:
            precond = pol_wide * residual
            rho_next = set_sums(residual, precond)
            search = precond + spread_sets(rho_next / rho_now) * search
            rho_now = rho_next
    return (dipoles, residual)
```

```python
import jax
import jax.numpy as jnp
from jax import lax
from jax.sharding import PartitionSpec as P

ITERS = 2


thole_factor = 0.39
column_width = 8.0
pair_batch = 8
slot_shift_x = (0.0, 0.0, 1.0, 1.0, 1.0)
slot_shift_y = (0.0, 1.0, -1.0, 0.0, 1.0)


def padded_2(cells, sides, width):
    for axis, dim in sides:
        count = lax.axis_size(axis)
        head = lax.slice_in_dim(cells, 0, width, axis=dim)
        tail = lax.slice_in_dim(cells, cells.shape[dim] - width, cells.shape[dim], axis=dim)
        cells = jnp.concatenate(
            [
                lax.ppermute(tail, axis, [(i, (i + 1) % count) for i in range(count)]),
                cells,
                lax.ppermute(head, axis, [((i + 1) % count, i) for i in range(count)]),
            ],
            axis=dim,
        )
    return cells


def from_behind(value, axis, steps):
    count = lax.axis_size(axis)
    pairs = [(source, (source + steps) % count) for source in range(count)]
    return lax.ppermute(value, axis, pairs)


def tensor_apply(coef_three, coef_five, deltas, moment, axis_sum):
    if axis_sum == 2:
        moments = [moment[:, member, None, :] for member in range(3)]
    else:
        moments = [moment[:, member, :, None] for member in range(3)]
    project = deltas[0] * moments[0] + deltas[1] * moments[1] + deltas[2] * moments[2]
    scaled = coef_five * project
    return jnp.stack(
        [
            jnp.sum(scaled * deltas[member] - coef_three * moments[member], axis=axis_sum)
            for member in range(3)
        ],
        axis=1,
    )


def pair_fields(geom_i, geom_j, dip_i, dip_j, slot_ids, same_block):
    chosen = (slot_ids[:, None] == jnp.arange(5, dtype=jnp.int32)[None, :]).astype(jnp.float32)
    offset_x = column_width * jnp.sum(
        chosen * jnp.array(slot_shift_x, jnp.float32)[None, :], axis=1
    )
    offset_y = column_width * jnp.sum(
        chosen * jnp.array(slot_shift_y, jnp.float32)[None, :], axis=1
    )
    delta_x = geom_j[:, 0, None, :] + offset_x[:, None, None] - geom_i[:, 0, :, None]
    delta_y = geom_j[:, 1, None, :] + offset_y[:, None, None] - geom_i[:, 1, :, None]
    delta_z = geom_j[:, 2, None, :] - geom_i[:, 2, :, None]
    dist_sq = delta_x * delta_x + delta_y * delta_y + delta_z * delta_z
    atom_width = geom_i.shape[2]
    same_atom = jnp.arange(atom_width)[:, None] == jnp.arange(atom_width)[None, :]
    diagonal = same_atom[None, :, :] & same_block[:, None, None]
    dist_sq = jnp.where(diagonal, 1.0, dist_sq)
    inv_dist = lax.rsqrt(dist_sq)
    inv_cube = inv_dist * inv_dist * inv_dist
    root_pol = jnp.sqrt(geom_i[:, 3, :, None] * geom_j[:, 3, None, :])
    damping = thole_factor * dist_sq * jnp.sqrt(dist_sq) / root_pol
    lambda_three = -jnp.expm1(-damping)
    lambda_five = lambda_three - damping * jnp.exp(-damping)
    keep_pair = jnp.where(diagonal, 0.0, 1.0)
    coef_three = keep_pair * lambda_three * inv_cube
    coef_five = keep_pair * 3.0 * lambda_five * inv_cube * inv_dist * inv_dist
    deltas = (delta_x, delta_y, delta_z)
    forward = jnp.concatenate(
        [
            tensor_apply(coef_three, coef_five, deltas, dip_j[:, 0:3], 2),
            tensor_apply(coef_three, coef_five, deltas, dip_j[:, 3:6], 2),
        ],
        axis=1,
    )
    backward = jnp.concatenate(
        [
            tensor_apply(coef_three, coef_five, deltas, dip_i[:, 0:3], 1),
            tensor_apply(coef_three, coef_five, deltas, dip_i[:, 3:6], 1),
        ],
        axis=1,
    )
    return (forward, backward)


def accumulate(geom_stack, dip_stack, entries, pair_total, live_turns, capacity_turns):
    blocks = geom_stack.shape[0] // 5
    atom_width = geom_stack.shape[2]
    targets = jnp.arange(5 * blocks, dtype=jnp.int32)
    padded = jnp.pad(entries, ((0, 0), (0, capacity_turns * pair_batch - entries.shape[1])))

    def one_turn(turn_index, accumulated):
        first_row = (turn_index * pair_batch).astype(jnp.int32)
        group_rows = lax.dynamic_slice_in_dim(padded, first_row, pair_batch, 1)
        own_block = group_rows[0]
        slot_ids = group_rows[1]
        other_block = group_rows[2]
        source = slot_ids * blocks + other_block
        live_rows = (first_row + jnp.arange(pair_batch, dtype=jnp.int32) < pair_total).astype(
            jnp.float32
        )
        same_block = (slot_ids == 0) & (own_block == other_block)
        forward, backward = pair_fields(
            jnp.take(geom_stack, own_block, axis=0),
            jnp.take(geom_stack, source, axis=0),
            jnp.take(dip_stack, own_block, axis=0),
            jnp.take(dip_stack, source, axis=0),
            slot_ids,
            same_block,
        )
        to_own = (own_block[:, None] == targets[None, :]).astype(jnp.float32) * live_rows[:, None]
        twoway = live_rows * (1.0 - same_block.astype(jnp.float32))
        to_other = (source[:, None] == targets[None, :]).astype(jnp.float32) * twoway[:, None]
        accumulated = accumulated + jnp.einsum(
            "gt,gca->tca", to_own, forward, precision=lax.Precision.HIGHEST
        )
        return accumulated + jnp.einsum(
            "gt,gca->tca", to_other, backward, precision=lax.Precision.HIGHEST
        )

    return lax.fori_loop(
        0, live_turns, one_turn, jnp.zeros((5 * blocks, 6, atom_width), jnp.float32)
    )


def neighbours(block_data):
    column = padded_2(block_data[None, None], (("gy", 1),), 1)
    across = from_behind(column, "gx", -1)
    return jnp.concatenate([block_data[None], column[0, 2:3], across[0]], axis=0)


def send_back(partials):
    received = from_behind(partials[None, 1:4], "gx", 1)
    paired = jnp.stack([received[0, 0], received[0, 2] + partials[0]], axis=0)[None]
    column = padded_2(paired, (("gy", 1),), 1)
    return column[0, 0] + column[0, 3] + received[0, 1]


def set_sums(first_vec, second_vec):
    product = (first_vec * second_vec).reshape(first_vec.shape[0], 2, 3, first_vec.shape[2])
    return jnp.sum(product, axis=(0, 2, 3))


def spread_sets(values):
    return jnp.repeat(values, 3)[None, :, None]


def global_sums(local_values):
    column = jnp.sum(lax.all_gather(local_values, "gy"), axis=0)
    return jnp.sum(lax.all_gather(column, "gx"), axis=0)


def per_device(positions, polarity, direct_field, atom_count, pair_list, pair_count):
    blocks = positions.shape[2]
    atom_width = positions.shape[4]
    atom_mask = (
        jnp.arange(atom_width, dtype=jnp.int32)[None, :] < atom_count[0, 0][:, None]
    ).astype(jnp.float32)
    pol_wide = polarity[0, 0][:, None, :]
    geometry = jnp.concatenate([positions[0, 0], pol_wide], axis=1)
    entries = pair_list[0, 0]
    pair_total = pair_count[0, 0]
    capacity_turns = -(-entries.shape[1] // pair_batch)
    live_turns = (pair_total + pair_batch - 1) // pair_batch

    def mutual_field(geom_stack, dip_stack):
        accumulated = accumulate(
            geom_stack, dip_stack, entries, pair_total, live_turns, capacity_turns
        )
        accumulated = accumulated.reshape(5, blocks, 6, atom_width)
        return (accumulated[0] + send_back(accumulated[1:5])) * atom_mask[:, None, :]

    residual = direct_field[0, 0] * atom_mask[:, None, :]
    search = pol_wide * residual
    stacked = neighbours(jnp.concatenate([geometry, search], axis=1))
    geom_stack = stacked[:, :, 0:4].reshape(5 * blocks, 4, atom_width)
    dip_stack = stacked[:, :, 4:10].reshape(5 * blocks, 6, atom_width)
    image = search / pol_wide - mutual_field(geom_stack, dip_stack)
    scaled = pol_wide * image
    scaled_dip = neighbours(scaled).reshape(5 * blocks, 6, atom_width)
    image_scaled = scaled / pol_wide - mutual_field(geom_stack, scaled_dip)
    first = global_sums(
        jnp.concatenate([set_sums(residual, search), set_sums(search, image)])
    )
    rho_now = first[0:2]
    curv_now = first[2:4]
    step_size = spread_sets(rho_now / curv_now)
    dipoles = step_size * search
    residual = residual - step_size * image
    precond = pol_wide * residual
    precond_image = image - step_size * image_scaled
    second = global_sums(
        jnp.concatenate(
            [
                set_sums(residual, precond),
                set_sums(precond, precond_image),
                set_sums(precond, image) + set_sums(search, precond_image),
            ]
        )
    )
    rho_next = second[0:2]
    ratio = rho_next / rho_now
    curv_next = second[2:4] + ratio * second[4:6] + ratio * ratio * curv_now
    ratio_wide = spread_sets(ratio)
    search = precond + ratio_wide * search
    image = precond_image + ratio_wide * image
    step_size = spread_sets(rho_next / curv_next)
    dipoles = dipoles + step_size * search
    residual = residual - step_size * image
    return (dipoles[None, None], residual[None, None])


def solution(mesh):
    in_specs = (
        P("gx", "gy", None, None, None),
        P("gx", "gy", None, None),
        P("gx", "gy", None, None, None),
        P("gx", "gy", None),
        P("gx", "gy", None, None),
        P("gx", "gy"),
    )
    out_specs = (P("gx", "gy", None, None, None), P("gx", "gy", None, None, None))
    return jax.shard_map(
        per_device, mesh=mesh, in_specs=in_specs, out_specs=out_specs, check_vma=False
    )
```

```python
import jax
import jax.numpy as jnp
from jax import lax
from jax.sharding import PartitionSpec as P

ITERS = 2


thole_factor = 0.39
column_width = 8.0
pair_batch = 8
slot_shift_x = (0.0, 0.0, 1.0, 1.0, 1.0)
slot_shift_y = (0.0, 1.0, -1.0, 0.0, 1.0)


def padded_2(cells, sides, width):
    for axis, dim in sides:
        count = lax.axis_size(axis)
        head = lax.slice_in_dim(cells, 0, width, axis=dim)
        tail = lax.slice_in_dim(cells, cells.shape[dim] - width, cells.shape[dim], axis=dim)
        cells = jnp.concatenate(
            [
                lax.ppermute(tail, axis, [(i, (i + 1) % count) for i in range(count)]),
                cells,
                lax.ppermute(head, axis, [((i + 1) % count, i) for i in range(count)]),
            ],
            axis=dim,
        )
    return cells


def from_behind(value, axis, steps):
    count = lax.axis_size(axis)
    pairs = [(source, (source + steps) % count) for source in range(count)]
    return lax.ppermute(value, axis, pairs)


def tensor_apply(coef_three, coef_five, deltas, moment, axis_sum):
    if axis_sum == 2:
        moments = [moment[:, member, None, :] for member in range(3)]
    else:
        moments = [moment[:, member, :, None] for member in range(3)]
    project = deltas[0] * moments[0] + deltas[1] * moments[1] + deltas[2] * moments[2]
    scaled = coef_five * project
    return jnp.stack(
        [
            jnp.sum(scaled * deltas[member] - coef_three * moments[member], axis=axis_sum)
            for member in range(3)
        ],
        axis=1,
    )


def pair_fields(geom_i, geom_j, dip_i, dip_j, slot_ids, same_block):
    chosen = (slot_ids[:, None] == jnp.arange(5, dtype=jnp.int32)[None, :]).astype(jnp.float32)
    offset_x = column_width * jnp.sum(
        chosen * jnp.array(slot_shift_x, jnp.float32)[None, :], axis=1
    )
    offset_y = column_width * jnp.sum(
        chosen * jnp.array(slot_shift_y, jnp.float32)[None, :], axis=1
    )
    delta_x = geom_j[:, 0, None, :] + offset_x[:, None, None] - geom_i[:, 0, :, None]
    delta_y = geom_j[:, 1, None, :] + offset_y[:, None, None] - geom_i[:, 1, :, None]
    delta_z = geom_j[:, 2, None, :] - geom_i[:, 2, :, None]
    dist_sq = delta_x * delta_x + delta_y * delta_y + delta_z * delta_z
    atom_width = geom_i.shape[2]
    same_atom = jnp.arange(atom_width)[:, None] == jnp.arange(atom_width)[None, :]
    diagonal = same_atom[None, :, :] & same_block[:, None, None]
    dist_sq = jnp.where(diagonal, 1.0, dist_sq)
    inv_dist = lax.rsqrt(dist_sq)
    inv_cube = inv_dist * inv_dist * inv_dist
    root_pol = jnp.sqrt(geom_i[:, 3, :, None] * geom_j[:, 3, None, :])
    damping = thole_factor * dist_sq * jnp.sqrt(dist_sq) / root_pol
    lambda_three = -jnp.expm1(-damping)
    lambda_five = lambda_three - damping * jnp.exp(-damping)
    keep_pair = jnp.where(diagonal, 0.0, 1.0)
    coef_three = keep_pair * lambda_three * inv_cube
    coef_five = keep_pair * 3.0 * lambda_five * inv_cube * inv_dist * inv_dist
    deltas = (delta_x, delta_y, delta_z)
    forward = jnp.concatenate(
        [
            tensor_apply(coef_three, coef_five, deltas, dip_j[:, 0:3], 2),
            tensor_apply(coef_three, coef_five, deltas, dip_j[:, 3:6], 2),
        ],
        axis=1,
    )
    backward = jnp.concatenate(
        [
            tensor_apply(coef_three, coef_five, deltas, dip_i[:, 0:3], 1),
            tensor_apply(coef_three, coef_five, deltas, dip_i[:, 3:6], 1),
        ],
        axis=1,
    )
    return (forward, backward)


def accumulate(geom_stack, dip_stack, entries, pair_total, live_turns, capacity_turns):
    blocks = geom_stack.shape[0] // 5
    atom_width = geom_stack.shape[2]
    targets = jnp.arange(5 * blocks, dtype=jnp.int32)
    padded = jnp.pad(entries, ((0, 0), (0, capacity_turns * pair_batch - entries.shape[1])))

    def one_turn(turn_index, accumulated):
        first_row = (turn_index * pair_batch).astype(jnp.int32)
        group_rows = lax.dynamic_slice_in_dim(padded, first_row, pair_batch, 1)
        own_block = group_rows[0]
        slot_ids = group_rows[1]
        other_block = group_rows[2]
        source = slot_ids * blocks + other_block
        live_rows = (first_row + jnp.arange(pair_batch, dtype=jnp.int32) < pair_total).astype(
            jnp.float32
        )
        same_block = (slot_ids == 0) & (own_block == other_block)
        forward, backward = pair_fields(
            jnp.take(geom_stack, own_block, axis=0),
            jnp.take(geom_stack, source, axis=0),
            jnp.take(dip_stack, own_block, axis=0),
            jnp.take(dip_stack, source, axis=0),
            slot_ids,
            same_block,
        )
        to_own = (own_block[:, None] == targets[None, :]).astype(jnp.float32) * live_rows[:, None]
        twoway = live_rows * (1.0 - same_block.astype(jnp.float32))
        to_other = (source[:, None] == targets[None, :]).astype(jnp.float32) * twoway[:, None]
        accumulated = accumulated + jnp.einsum(
            "gt,gca->tca", to_own, forward, precision=lax.Precision.HIGHEST
        )
        return accumulated + jnp.einsum(
            "gt,gca->tca", to_other, backward, precision=lax.Precision.HIGHEST
        )

    return lax.fori_loop(
        0, live_turns, one_turn, jnp.zeros((5 * blocks, 6, atom_width), jnp.float32)
    )


def neighbours(block_data):
    column = padded_2(block_data[None, None], (("gy", 1),), 1)
    across = from_behind(column, "gx", -1)
    return jnp.concatenate([block_data[None], column[0, 2:3], across[0]], axis=0)


def send_back(partials):
    received = from_behind(partials[None, 1:4], "gx", 1)
    paired = jnp.stack([received[0, 0], received[0, 2] + partials[0]], axis=0)[None]
    column = padded_2(paired, (("gy", 1),), 1)
    return column[0, 0] + column[0, 3] + received[0, 1]


def set_sums(first_vec, second_vec):
    product = (first_vec * second_vec).reshape(first_vec.shape[0], 2, 3, first_vec.shape[2])
    return jnp.sum(product, axis=(0, 2, 3))


def spread_sets(values):
    return jnp.repeat(values, 3)[None, :, None]


def global_sums(local_values):
    column = jnp.sum(lax.all_gather(local_values, "gy"), axis=0)
    return jnp.sum(lax.all_gather(column, "gx"), axis=0)


def per_device(positions, polarity, direct_field, atom_count, pair_list, pair_count):
    blocks = positions.shape[2]
    atom_width = positions.shape[4]
    atom_mask = (
        jnp.arange(atom_width, dtype=jnp.int32)[None, :] < atom_count[0, 0][:, None]
    ).astype(jnp.float32)
    pol_wide = polarity[0, 0][:, None, :]
    geometry = jnp.concatenate([positions[0, 0], pol_wide], axis=1)
    entries = pair_list[0, 0]
    pair_total = pair_count[0, 0]
    capacity_turns = -(-entries.shape[1] // pair_batch)
    live_turns = (pair_total + pair_batch - 1) // pair_batch

    def mutual_field(geom_stack, dip_stack):
        accumulated = accumulate(
            geom_stack, dip_stack, entries, pair_total, live_turns, capacity_turns
        )
        accumulated = accumulated.reshape(5, blocks, 6, atom_width)
        return (accumulated[0] + send_back(accumulated[1:5])) * atom_mask[:, None, :]

    residual = direct_field[0, 0] * atom_mask[:, None, :]
    search = pol_wide * residual
    stacked = neighbours(jnp.concatenate([geometry, search], axis=1))
    geom_stack = stacked[:, :, 0:4].reshape(5 * blocks, 4, atom_width)
    dip_stack = stacked[:, :, 4:10].reshape(5 * blocks, 6, atom_width)
    image = search / pol_wide - mutual_field(geom_stack, dip_stack)
    scaled = pol_wide * image
    scaled_dip = neighbours(scaled).reshape(5 * blocks, 6, atom_width)
    image_scaled = scaled / pol_wide - mutual_field(geom_stack, scaled_dip)
    sums = global_sums(
        jnp.concatenate(
            [
                set_sums(residual, search),
                set_sums(search, image),
                set_sums(image, scaled),
                set_sums(search, image_scaled),
                set_sums(scaled, image_scaled),
            ]
        )
    )
    rho_now = sums[0:2]
    curv_now = sums[2:4]
    image_pre = sums[4:6]
    search_cross = sums[6:8]
    scaled_curv = sums[8:10]
    step_now = rho_now / curv_now
    step_size = spread_sets(step_now)
    dipoles = step_size * search
    residual = residual - step_size * image
    precond = pol_wide * residual
    precond_image = image - step_size * image_scaled
    rho_next = rho_now - 2.0 * step_now * curv_now + step_now * step_now * image_pre
    mixed = image_pre + search_cross
    precond_curv = curv_now - step_now * mixed + step_now * step_now * scaled_curv
    cross = 2.0 * curv_now - step_now * mixed
    ratio = rho_next / rho_now
    curv_next = precond_curv + ratio * cross + ratio * ratio * curv_now
    ratio_wide = spread_sets(ratio)
    search = precond + ratio_wide * search
    image = precond_image + ratio_wide * image
    step_size = spread_sets(rho_next / curv_next)
    dipoles = dipoles + step_size * search
    residual = residual - step_size * image
    return (dipoles[None, None], residual[None, None])


def solution(mesh):
    in_specs = (
        P("gx", "gy", None, None, None),
        P("gx", "gy", None, None),
        P("gx", "gy", None, None, None),
        P("gx", "gy", None),
        P("gx", "gy", None, None),
        P("gx", "gy"),
    )
    out_specs = (P("gx", "gy", None, None, None), P("gx", "gy", None, None, None))
    return jax.shard_map(
        per_device, mesh=mesh, in_specs=in_specs, out_specs=out_specs, check_vma=False
    )
```

```python
import jax
import jax.numpy as jnp
from jax import lax
from jax.sharding import PartitionSpec as P

ITERS = 2


thole_factor = 0.39
column_width = 8.0
pair_batch = 8
slot_shift_x = (0.0, 0.0, 1.0, 1.0, 1.0)
slot_shift_y = (0.0, 1.0, -1.0, 0.0, 1.0)


def padded_2(cells, sides, width):
    for axis, dim in sides:
        count = lax.axis_size(axis)
        head = lax.slice_in_dim(cells, 0, width, axis=dim)
        tail = lax.slice_in_dim(cells, cells.shape[dim] - width, cells.shape[dim], axis=dim)
        cells = jnp.concatenate(
            [
                lax.ppermute(tail, axis, [(i, (i + 1) % count) for i in range(count)]),
                cells,
                lax.ppermute(head, axis, [((i + 1) % count, i) for i in range(count)]),
            ],
            axis=dim,
        )
    return cells


def from_behind(value, axis, steps):
    count = lax.axis_size(axis)
    pairs = [(source, (source + steps) % count) for source in range(count)]
    return lax.ppermute(value, axis, pairs)


def tensor_apply(coef_three, coef_five, deltas, moment, axis_sum):
    if axis_sum == 2:
        moments = [moment[:, member, None, :] for member in range(3)]
    else:
        moments = [moment[:, member, :, None] for member in range(3)]
    project = deltas[0] * moments[0] + deltas[1] * moments[1] + deltas[2] * moments[2]
    scaled = coef_five * project
    return jnp.stack(
        [
            jnp.sum(scaled * deltas[member] - coef_three * moments[member], axis=axis_sum)
            for member in range(3)
        ],
        axis=1,
    )


def pair_fields(geom_i, geom_j, dip_i, dip_j, slot_ids, same_block):
    chosen = (slot_ids[:, None] == jnp.arange(5, dtype=jnp.int32)[None, :]).astype(jnp.float32)
    offset_x = column_width * jnp.sum(
        chosen * jnp.array(slot_shift_x, jnp.float32)[None, :], axis=1
    )
    offset_y = column_width * jnp.sum(
        chosen * jnp.array(slot_shift_y, jnp.float32)[None, :], axis=1
    )
    delta_x = geom_j[:, 0, None, :] + offset_x[:, None, None] - geom_i[:, 0, :, None]
    delta_y = geom_j[:, 1, None, :] + offset_y[:, None, None] - geom_i[:, 1, :, None]
    delta_z = geom_j[:, 2, None, :] - geom_i[:, 2, :, None]
    dist_sq = delta_x * delta_x + delta_y * delta_y + delta_z * delta_z
    atom_width = geom_i.shape[2]
    same_atom = jnp.arange(atom_width)[:, None] == jnp.arange(atom_width)[None, :]
    diagonal = same_atom[None, :, :] & same_block[:, None, None]
    dist_sq = jnp.where(diagonal, 1.0, dist_sq)
    inv_dist = lax.rsqrt(dist_sq)
    inv_cube = inv_dist * inv_dist * inv_dist
    root_pol = jnp.sqrt(geom_i[:, 3, :, None] * geom_j[:, 3, None, :])
    damping = thole_factor * dist_sq * jnp.sqrt(dist_sq) / root_pol
    lambda_three = -jnp.expm1(-damping)
    lambda_five = lambda_three - damping * jnp.exp(-damping)
    keep_pair = jnp.where(diagonal, 0.0, 1.0)
    coef_three = keep_pair * lambda_three * inv_cube
    coef_five = keep_pair * 3.0 * lambda_five * inv_cube * inv_dist * inv_dist
    deltas = (delta_x, delta_y, delta_z)
    forward = jnp.concatenate(
        [
            tensor_apply(coef_three, coef_five, deltas, dip_j[:, 0:3], 2),
            tensor_apply(coef_three, coef_five, deltas, dip_j[:, 3:6], 2),
        ],
        axis=1,
    )
    backward = jnp.concatenate(
        [
            tensor_apply(coef_three, coef_five, deltas, dip_i[:, 0:3], 1),
            tensor_apply(coef_three, coef_five, deltas, dip_i[:, 3:6], 1),
        ],
        axis=1,
    )
    return (forward, backward)


def accumulate(geom_stack, dip_stack, entries, pair_total, live_turns, capacity_turns):
    blocks = geom_stack.shape[0] // 5
    atom_width = geom_stack.shape[2]
    targets = jnp.arange(5 * blocks, dtype=jnp.int32)
    padded = jnp.pad(entries, ((0, 0), (0, capacity_turns * pair_batch - entries.shape[1])))

    def one_turn(turn_index, accumulated):
        first_row = (turn_index * pair_batch).astype(jnp.int32)
        group_rows = lax.dynamic_slice_in_dim(padded, first_row, pair_batch, 1)
        own_block = group_rows[0]
        slot_ids = group_rows[1]
        other_block = group_rows[2]
        source = slot_ids * blocks + other_block
        live_rows = (first_row + jnp.arange(pair_batch, dtype=jnp.int32) < pair_total).astype(
            jnp.float32
        )
        same_block = (slot_ids == 0) & (own_block == other_block)
        forward, backward = pair_fields(
            jnp.take(geom_stack, own_block, axis=0),
            jnp.take(geom_stack, source, axis=0),
            jnp.take(dip_stack, own_block, axis=0),
            jnp.take(dip_stack, source, axis=0),
            slot_ids,
            same_block,
        )
        to_own = (own_block[:, None] == targets[None, :]).astype(jnp.float32) * live_rows[:, None]
        twoway = live_rows * (1.0 - same_block.astype(jnp.float32))
        to_other = (source[:, None] == targets[None, :]).astype(jnp.float32) * twoway[:, None]
        accumulated = accumulated + jnp.einsum(
            "gt,gca->tca", to_own, forward, precision=lax.Precision.HIGHEST
        )
        return accumulated + jnp.einsum(
            "gt,gca->tca", to_other, backward, precision=lax.Precision.HIGHEST
        )

    return lax.fori_loop(
        0, live_turns, one_turn, jnp.zeros((5 * blocks, 6, atom_width), jnp.float32)
    )


def neighbours(block_data):
    column = padded_2(block_data[None, None], (("gy", 1),), 1)
    across = from_behind(column, "gx", -1)
    return jnp.concatenate([block_data[None], column[0, 2:3], across[0]], axis=0)


def send_back(partials):
    received = from_behind(partials[None, 1:4], "gx", 1)
    paired = jnp.stack([received[0, 0], received[0, 2] + partials[0]], axis=0)[None]
    column = padded_2(paired, (("gy", 1),), 1)
    return column[0, 0] + column[0, 3] + received[0, 1]


def set_sums(first_vec, second_vec):
    product = (first_vec * second_vec).reshape(first_vec.shape[0], 2, 3, first_vec.shape[2])
    return jnp.sum(product, axis=(0, 2, 3))


def spread_sets(values):
    return jnp.repeat(values, 3)[None, :, None]


def global_sums(local_values):
    return lax.psum(local_values, ("gx", "gy"))


def per_device(positions, polarity, direct_field, atom_count, pair_list, pair_count):
    blocks = positions.shape[2]
    atom_width = positions.shape[4]
    atom_mask = (
        jnp.arange(atom_width, dtype=jnp.int32)[None, :] < atom_count[0, 0][:, None]
    ).astype(jnp.float32)
    pol_wide = polarity[0, 0][:, None, :]
    geometry = jnp.concatenate([positions[0, 0], pol_wide], axis=1)
    entries = pair_list[0, 0]
    pair_total = pair_count[0, 0]
    capacity_turns = -(-entries.shape[1] // pair_batch)
    live_turns = (pair_total + pair_batch - 1) // pair_batch

    def mutual_field(geom_stack, dip_stack):
        accumulated = accumulate(
            geom_stack, dip_stack, entries, pair_total, live_turns, capacity_turns
        )
        accumulated = accumulated.reshape(5, blocks, 6, atom_width)
        return (accumulated[0] + send_back(accumulated[1:5])) * atom_mask[:, None, :]

    residual = direct_field[0, 0] * atom_mask[:, None, :]
    search = pol_wide * residual
    stacked = neighbours(jnp.concatenate([geometry, search], axis=1))
    geom_stack = stacked[:, :, 0:4].reshape(5 * blocks, 4, atom_width)
    dip_stack = stacked[:, :, 4:10].reshape(5 * blocks, 6, atom_width)
    image = search / pol_wide - mutual_field(geom_stack, dip_stack)
    scaled = pol_wide * image
    scaled_dip = neighbours(scaled).reshape(5 * blocks, 6, atom_width)
    image_scaled = scaled / pol_wide - mutual_field(geom_stack, scaled_dip)
    sums = global_sums(
        jnp.concatenate(
            [
                set_sums(residual, search),
                set_sums(search, image),
                set_sums(image, scaled),
                set_sums(search, image_scaled),
                set_sums(scaled, image_scaled),
            ]
        )
    )
    rho_now = sums[0:2]
    curv_now = sums[2:4]
    image_pre = sums[4:6]
    search_cross = sums[6:8]
    scaled_curv = sums[8:10]
    step_now = rho_now / curv_now
    step_size = spread_sets(step_now)
    dipoles = step_size * search
    residual = residual - step_size * image
    precond = pol_wide * residual
    precond_image = image - step_size * image_scaled
    rho_next = rho_now - 2.0 * step_now * curv_now + step_now * step_now * image_pre
    mixed = image_pre + search_cross
    precond_curv = curv_now - step_now * mixed + step_now * step_now * scaled_curv
    cross = 2.0 * curv_now - step_now * mixed
    ratio = rho_next / rho_now
    curv_next = precond_curv + ratio * cross + ratio * ratio * curv_now
    ratio_wide = spread_sets(ratio)
    search = precond + ratio_wide * search
    image = precond_image + ratio_wide * image
    step_size = spread_sets(rho_next / curv_next)
    dipoles = dipoles + step_size * search
    residual = residual - step_size * image
    return (dipoles[None, None], residual[None, None])


def solution(mesh):
    in_specs = (
        P("gx", "gy", None, None, None),
        P("gx", "gy", None, None),
        P("gx", "gy", None, None, None),
        P("gx", "gy", None),
        P("gx", "gy", None, None),
        P("gx", "gy"),
    )
    out_specs = (P("gx", "gy", None, None, None), P("gx", "gy", None, None, None))
    return jax.shard_map(
        per_device, mesh=mesh, in_specs=in_specs, out_specs=out_specs, check_vma=False
    )
```

```python
import jax
import jax.numpy as jnp
from jax import lax
from jax.sharding import PartitionSpec as P

ITERS = 2


thole_factor = 0.39
column_width = 8.0
slot_shift_x = (0.0, 0.0, 1.0, 1.0, 1.0)
slot_shift_y = (0.0, 1.0, -1.0, 0.0, 1.0)


def padded_2(cells, sides, width):
    for axis, dim in sides:
        count = lax.axis_size(axis)
        head = lax.slice_in_dim(cells, 0, width, axis=dim)
        tail = lax.slice_in_dim(cells, cells.shape[dim] - width, cells.shape[dim], axis=dim)
        cells = jnp.concatenate(
            [
                lax.ppermute(tail, axis, [(i, (i + 1) % count) for i in range(count)]),
                cells,
                lax.ppermute(head, axis, [((i + 1) % count, i) for i in range(count)]),
            ],
            axis=dim,
        )
    return cells


def from_behind(value, axis, steps):
    count = lax.axis_size(axis)
    pairs = [(source, (source + steps) % count) for source in range(count)]
    return lax.ppermute(value, axis, pairs)


def tensor_apply(coef_three, coef_five, deltas, moment, axis_sum):
    if axis_sum == 2:
        moments = [moment[:, member, None, :] for member in range(3)]
    else:
        moments = [moment[:, member, :, None] for member in range(3)]
    project = deltas[0] * moments[0] + deltas[1] * moments[1] + deltas[2] * moments[2]
    scaled = coef_five * project
    return jnp.stack(
        [
            jnp.sum(scaled * deltas[member] - coef_three * moments[member], axis=axis_sum)
            for member in range(3)
        ],
        axis=1,
    )


def pair_fields(geom_i, geom_j, dip_i, dip_j, slot_ids, same_block, two_way=True):
    chosen = (slot_ids[:, None] == jnp.arange(5, dtype=jnp.int32)[None, :]).astype(jnp.float32)
    offset_x = column_width * jnp.sum(
        chosen * jnp.array(slot_shift_x, jnp.float32)[None, :], axis=1
    )
    offset_y = column_width * jnp.sum(
        chosen * jnp.array(slot_shift_y, jnp.float32)[None, :], axis=1
    )
    delta_x = geom_j[:, 0, None, :] + offset_x[:, None, None] - geom_i[:, 0, :, None]
    delta_y = geom_j[:, 1, None, :] + offset_y[:, None, None] - geom_i[:, 1, :, None]
    delta_z = geom_j[:, 2, None, :] - geom_i[:, 2, :, None]
    dist_sq = delta_x * delta_x + delta_y * delta_y + delta_z * delta_z
    atom_width = geom_i.shape[2]
    same_atom = jnp.arange(atom_width)[:, None] == jnp.arange(atom_width)[None, :]
    diagonal = same_atom[None, :, :] & same_block[:, None, None]
    dist_sq = jnp.where(diagonal, 1.0, dist_sq)
    inv_dist = lax.rsqrt(dist_sq)
    inv_cube = inv_dist * inv_dist * inv_dist
    root_pol = jnp.sqrt(geom_i[:, 3, :, None] * geom_j[:, 3, None, :])
    damping = thole_factor * dist_sq * jnp.sqrt(dist_sq) / root_pol
    lambda_three = -jnp.expm1(-damping)
    lambda_five = lambda_three - damping * jnp.exp(-damping)
    keep_pair = jnp.where(diagonal, 0.0, 1.0)
    coef_three = keep_pair * lambda_three * inv_cube
    coef_five = keep_pair * 3.0 * lambda_five * inv_cube * inv_dist * inv_dist
    deltas = (delta_x, delta_y, delta_z)
    forward = jnp.concatenate(
        [
            tensor_apply(coef_three, coef_five, deltas, dip_j[:, 0:3], 2),
            tensor_apply(coef_three, coef_five, deltas, dip_j[:, 3:6], 2),
        ],
        axis=1,
    )
    if not two_way:
        return (forward, None)
    backward = jnp.concatenate(
        [
            tensor_apply(coef_three, coef_five, deltas, dip_i[:, 0:3], 1),
            tensor_apply(coef_three, coef_five, deltas, dip_i[:, 3:6], 1),
        ],
        axis=1,
    )
    return (forward, backward)


def pair_presence(entries, pair_total, blocks):
    live = jnp.arange(entries.shape[1], dtype=jnp.int32) < pair_total
    own_block, slot_ids, other_block = entries[0], entries[1], entries[2]
    shift = other_block - own_block + 1
    hit = (
        live[:, None, None, None]
        & (slot_ids[:, None, None, None] == jnp.arange(5, dtype=jnp.int32)[None, :, None, None])
        & (shift[:, None, None, None] == jnp.arange(3, dtype=jnp.int32)[None, None, :, None])
        & (own_block[:, None, None, None] == jnp.arange(blocks, dtype=jnp.int32)[None, None, None, :])
    )
    return jnp.sum(hit.astype(jnp.float32), axis=0)


def shifted_batch(own, other, blocks):
    first = jnp.concatenate([own[1:blocks], own, own[0 : blocks - 1]], axis=0)
    second = jnp.concatenate([other[0 : blocks - 1], other, other[1:blocks]], axis=0)
    return first, second


def gated(values, present):
    return jnp.where(present[:, None, None] > 0, values, 0.0)


def accumulate(geom_stack, dip_stack, presence):
    blocks = geom_stack.shape[1]
    geom_own = geom_stack[0]
    dip_own = dip_stack[0]
    same, _ = pair_fields(
        geom_own,
        geom_own,
        dip_own,
        dip_own,
        jnp.zeros((blocks,), jnp.int32),
        jnp.ones((blocks,), bool),
        two_way=False,
    )
    own_total = gated(same, presence[0, 1])
    count = blocks - 1
    forward, backward = pair_fields(
        geom_own[0:count],
        geom_own[1:blocks],
        dip_own[0:count],
        dip_own[1:blocks],
        jnp.zeros((count,), jnp.int32),
        jnp.zeros((count,), bool),
    )
    near = presence[0, 2, 0:count]
    zero_block = jnp.zeros_like(own_total[0:1])
    own_total = own_total + jnp.concatenate([gated(forward, near), zero_block], axis=0)
    own_total = own_total + jnp.concatenate([zero_block, gated(backward, near)], axis=0)
    own_i, _ = shifted_batch(geom_own, geom_own, blocks)
    dip_i, _ = shifted_batch(dip_own, dip_own, blocks)
    width = 3 * blocks - 2

    def one_slot(slot_index, carry):
        own_acc, other_acc = carry
        geom_j = lax.dynamic_index_in_dim(geom_stack, slot_index, 0, keepdims=False)
        dip_j = lax.dynamic_index_in_dim(dip_stack, slot_index, 0, keepdims=False)
        _, geom_j = shifted_batch(geom_j, geom_j, blocks)
        _, dip_j = shifted_batch(dip_j, dip_j, blocks)
        listed = lax.dynamic_index_in_dim(presence, slot_index, 0, keepdims=False)
        present = jnp.concatenate([listed[0, 1:blocks], listed[1], listed[2, 0:count]])
        forward, backward = pair_fields(
            own_i,
            geom_j,
            dip_i,
            dip_j,
            jnp.full((width,), slot_index, jnp.int32),
            jnp.zeros((width,), bool),
        )
        forward = gated(forward, present)
        backward = gated(backward, present)
        own_acc = (
            own_acc
            + jnp.concatenate([zero_block, forward[0:count]], axis=0)
            + forward[count : count + blocks]
            + jnp.concatenate([forward[count + blocks : width], zero_block], axis=0)
        )
        other_sum = (
            jnp.concatenate([backward[0:count], zero_block], axis=0)
            + backward[count : count + blocks]
            + jnp.concatenate([zero_block, backward[count + blocks : width]], axis=0)
        )
        other_acc = lax.dynamic_update_index_in_dim(other_acc, other_sum, slot_index - 1, 0)
        return own_acc, other_acc

    other_acc = jnp.zeros((4,) + own_total.shape, jnp.float32)
    return lax.fori_loop(1, 5, one_slot, (own_total, other_acc))


def neighbours(block_data):
    column = padded_2(block_data[None, None], (("gy", 1),), 1)
    across = from_behind(column, "gx", -1)
    return jnp.concatenate([block_data[None], column[0, 2:3], across[0]], axis=0)


def send_back(partials):
    received = from_behind(partials[None, 1:4], "gx", 1)
    paired = jnp.stack([received[0, 0], received[0, 2] + partials[0]], axis=0)[None]
    column = padded_2(paired, (("gy", 1),), 1)
    return column[0, 0] + column[0, 3] + received[0, 1]


def set_sums(first_vec, second_vec):
    product = (first_vec * second_vec).reshape(first_vec.shape[0], 2, 3, first_vec.shape[2])
    return jnp.sum(product, axis=(0, 2, 3))


def spread_sets(values):
    return jnp.repeat(values, 3)[None, :, None]


def global_sums(local_values):
    return lax.psum(local_values, ("gx", "gy"))


def per_device(positions, polarity, direct_field, atom_count, pair_list, pair_count):
    blocks = positions.shape[2]
    atom_width = positions.shape[4]
    atom_mask = (
        jnp.arange(atom_width, dtype=jnp.int32)[None, :] < atom_count[0, 0][:, None]
    ).astype(jnp.float32)
    pol_wide = polarity[0, 0][:, None, :]
    geometry = jnp.concatenate([positions[0, 0], pol_wide], axis=1)
    entries = pair_list[0, 0]
    pair_total = pair_count[0, 0]
    presence = pair_presence(entries, pair_total, blocks)

    def mutual_field(geom_stack, dip_stack):
        own_total, other_acc = accumulate(geom_stack, dip_stack, presence)
        return (own_total + send_back(other_acc)) * atom_mask[:, None, :]

    residual = direct_field[0, 0] * atom_mask[:, None, :]
    search = pol_wide * residual
    stacked = neighbours(jnp.concatenate([geometry, search], axis=1))
    geom_stack = stacked[:, :, 0:4]
    dip_stack = stacked[:, :, 4:10]
    image = search / pol_wide - mutual_field(geom_stack, dip_stack)
    scaled = pol_wide * image
    scaled_dip = neighbours(scaled)
    image_scaled = scaled / pol_wide - mutual_field(geom_stack, scaled_dip)
    sums = global_sums(
        jnp.concatenate(
            [
                set_sums(residual, search),
                set_sums(search, image),
                set_sums(image, scaled),
                set_sums(search, image_scaled),
                set_sums(scaled, image_scaled),
            ]
        )
    )
    rho_now = sums[0:2]
    curv_now = sums[2:4]
    image_pre = sums[4:6]
    search_cross = sums[6:8]
    scaled_curv = sums[8:10]
    step_now = rho_now / curv_now
    step_size = spread_sets(step_now)
    dipoles = step_size * search
    residual = residual - step_size * image
    precond = pol_wide * residual
    precond_image = image - step_size * image_scaled
    rho_next = rho_now - 2.0 * step_now * curv_now + step_now * step_now * image_pre
    mixed = image_pre + search_cross
    precond_curv = curv_now - step_now * mixed + step_now * step_now * scaled_curv
    cross = 2.0 * curv_now - step_now * mixed
    ratio = rho_next / rho_now
    curv_next = precond_curv + ratio * cross + ratio * ratio * curv_now
    ratio_wide = spread_sets(ratio)
    search = precond + ratio_wide * search
    image = precond_image + ratio_wide * image
    step_size = spread_sets(rho_next / curv_next)
    dipoles = dipoles + step_size * search
    residual = residual - step_size * image
    return (dipoles[None, None], residual[None, None])


def solution(mesh):
    in_specs = (
        P("gx", "gy", None, None, None),
        P("gx", "gy", None, None),
        P("gx", "gy", None, None, None),
        P("gx", "gy", None),
        P("gx", "gy", None, None),
        P("gx", "gy"),
    )
    out_specs = (P("gx", "gy", None, None, None), P("gx", "gy", None, None, None))
    return jax.shard_map(
        per_device, mesh=mesh, in_specs=in_specs, out_specs=out_specs, check_vma=False
    )
```

```python
import jax
import jax.numpy as jnp
from jax import lax
from jax.sharding import PartitionSpec as P

ITERS = 2


thole_factor = 0.39
column_width = 8.0
slot_shift_x = (0.0, 0.0, 1.0, 1.0, 1.0)
slot_shift_y = (0.0, 1.0, -1.0, 0.0, 1.0)


def padded_2(cells, sides, width):
    for axis, dim in sides:
        count = lax.axis_size(axis)
        head = lax.slice_in_dim(cells, 0, width, axis=dim)
        tail = lax.slice_in_dim(cells, cells.shape[dim] - width, cells.shape[dim], axis=dim)
        cells = jnp.concatenate(
            [
                lax.ppermute(tail, axis, [(i, (i + 1) % count) for i in range(count)]),
                cells,
                lax.ppermute(head, axis, [((i + 1) % count, i) for i in range(count)]),
            ],
            axis=dim,
        )
    return cells


def from_behind(value, axis, steps):
    count = lax.axis_size(axis)
    pairs = [(source, (source + steps) % count) for source in range(count)]
    return lax.ppermute(value, axis, pairs)


def tensor_apply(coef_three, coef_five, deltas, moment, axis_sum):
    if axis_sum == 2:
        moments = [moment[:, member, None, :] for member in range(3)]
    else:
        moments = [moment[:, member, :, None] for member in range(3)]
    project = deltas[0] * moments[0] + deltas[1] * moments[1] + deltas[2] * moments[2]
    scaled = coef_five * project
    return jnp.stack(
        [
            jnp.sum(scaled * deltas[member] - coef_three * moments[member], axis=axis_sum)
            for member in range(3)
        ],
        axis=1,
    )


def pair_fields(geom_i, geom_j, dip_i, dip_j, slot_ids, same_block, two_way=True):
    chosen = (slot_ids[:, None] == jnp.arange(5, dtype=jnp.int32)[None, :]).astype(jnp.float32)
    offset_x = column_width * jnp.sum(
        chosen * jnp.array(slot_shift_x, jnp.float32)[None, :], axis=1
    )
    offset_y = column_width * jnp.sum(
        chosen * jnp.array(slot_shift_y, jnp.float32)[None, :], axis=1
    )
    delta_x = geom_j[:, 0, None, :] + offset_x[:, None, None] - geom_i[:, 0, :, None]
    delta_y = geom_j[:, 1, None, :] + offset_y[:, None, None] - geom_i[:, 1, :, None]
    delta_z = geom_j[:, 2, None, :] - geom_i[:, 2, :, None]
    dist_sq = delta_x * delta_x + delta_y * delta_y + delta_z * delta_z
    atom_width = geom_i.shape[2]
    same_atom = jnp.arange(atom_width)[:, None] == jnp.arange(atom_width)[None, :]
    diagonal = same_atom[None, :, :] & same_block[:, None, None]
    dist_sq = jnp.where(diagonal, 1.0, dist_sq)
    inv_dist = lax.rsqrt(dist_sq)
    inv_cube = inv_dist * inv_dist * inv_dist
    root_pol = jnp.sqrt(geom_i[:, 3, :, None] * geom_j[:, 3, None, :])
    damping = thole_factor * dist_sq * jnp.sqrt(dist_sq) / root_pol
    lambda_three = -jnp.expm1(-damping)
    lambda_five = lambda_three - damping * jnp.exp(-damping)
    keep_pair = jnp.where(diagonal, 0.0, 1.0)
    coef_three = keep_pair * lambda_three * inv_cube
    coef_five = keep_pair * 3.0 * lambda_five * inv_cube * inv_dist * inv_dist
    deltas = (delta_x, delta_y, delta_z)
    forward = jnp.concatenate(
        [
            tensor_apply(coef_three, coef_five, deltas, dip_j[:, 0:3], 2),
            tensor_apply(coef_three, coef_five, deltas, dip_j[:, 3:6], 2),
        ],
        axis=1,
    )
    if not two_way:
        return (forward, None)
    backward = jnp.concatenate(
        [
            tensor_apply(coef_three, coef_five, deltas, dip_i[:, 0:3], 1),
            tensor_apply(coef_three, coef_five, deltas, dip_i[:, 3:6], 1),
        ],
        axis=1,
    )
    return (forward, backward)


def pair_presence(entries, pair_total, blocks):
    live = jnp.arange(entries.shape[1], dtype=jnp.int32) < pair_total
    own_block, slot_ids, other_block = entries[0], entries[1], entries[2]
    shift = other_block - own_block + 1
    hit = (
        live[:, None, None, None]
        & (slot_ids[:, None, None, None] == jnp.arange(5, dtype=jnp.int32)[None, :, None, None])
        & (shift[:, None, None, None] == jnp.arange(3, dtype=jnp.int32)[None, None, :, None])
        & (own_block[:, None, None, None] == jnp.arange(blocks, dtype=jnp.int32)[None, None, None, :])
    )
    return jnp.sum(hit.astype(jnp.float32), axis=0)


def shifted_batch(own, other, blocks):
    first = jnp.concatenate([own[1:blocks], own, own[0 : blocks - 1]], axis=0)
    second = jnp.concatenate([other[0 : blocks - 1], other, other[1:blocks]], axis=0)
    return first, second


def gated(values, present):
    return jnp.where(present[:, None, None] > 0, values, 0.0)


def accumulate(geom_stack, dip_stack, presence):
    blocks = geom_stack.shape[1]
    geom_own = geom_stack[0]
    dip_own = dip_stack[0]
    same, _ = pair_fields(
        geom_own,
        geom_own,
        dip_own,
        dip_own,
        jnp.zeros((blocks,), jnp.int32),
        jnp.ones((blocks,), bool),
        two_way=False,
    )
    own_total = gated(same, presence[0, 1])
    count = blocks - 1
    forward, backward = pair_fields(
        geom_own[0:count],
        geom_own[1:blocks],
        dip_own[0:count],
        dip_own[1:blocks],
        jnp.zeros((count,), jnp.int32),
        jnp.zeros((count,), bool),
    )
    near = presence[0, 2, 0:count]
    zero_block = jnp.zeros_like(own_total[0:1])
    own_total = own_total + jnp.concatenate([gated(forward, near), zero_block], axis=0)
    own_total = own_total + jnp.concatenate([zero_block, gated(backward, near)], axis=0)
    own_i, _ = shifted_batch(geom_own, geom_own, blocks)
    dip_i, _ = shifted_batch(dip_own, dip_own, blocks)
    width = 3 * blocks - 2

    def one_slot(slot_index, carry):
        own_acc, other_acc = carry
        geom_j = lax.dynamic_index_in_dim(geom_stack, slot_index, 0, keepdims=False)
        dip_j = lax.dynamic_index_in_dim(dip_stack, slot_index, 0, keepdims=False)
        _, geom_j = shifted_batch(geom_j, geom_j, blocks)
        _, dip_j = shifted_batch(dip_j, dip_j, blocks)
        listed = lax.dynamic_index_in_dim(presence, slot_index, 0, keepdims=False)
        present = jnp.concatenate([listed[0, 1:blocks], listed[1], listed[2, 0:count]])
        forward, backward = pair_fields(
            own_i,
            geom_j,
            dip_i,
            dip_j,
            jnp.full((width,), slot_index, jnp.int32),
            jnp.zeros((width,), bool),
        )
        forward = gated(forward, present)
        backward = gated(backward, present)
        own_acc = (
            own_acc
            + jnp.concatenate([zero_block, forward[0:count]], axis=0)
            + forward[count : count + blocks]
            + jnp.concatenate([forward[count + blocks : width], zero_block], axis=0)
        )
        other_sum = (
            jnp.concatenate([backward[0:count], zero_block], axis=0)
            + backward[count : count + blocks]
            + jnp.concatenate([zero_block, backward[count + blocks : width]], axis=0)
        )
        other_acc = lax.dynamic_update_index_in_dim(other_acc, other_sum, slot_index - 1, 0)
        return own_acc, other_acc

    other_acc = jnp.zeros((4,) + own_total.shape, jnp.float32)
    return lax.fori_loop(1, 5, one_slot, (own_total, other_acc))


def neighbours(block_data):
    column = padded_2(block_data[None, None], (("gy", 1),), 1)
    across = from_behind(column, "gx", -1)
    return jnp.concatenate([block_data[None], column[0, 2:3], across[0]], axis=0)


def send_back(partials):
    received = from_behind(partials[None, 1:4], "gx", 1)
    paired = jnp.stack([received[0, 0], received[0, 2] + partials[0]], axis=0)[None]
    column = padded_2(paired, (("gy", 1),), 1)
    return column[0, 0] + column[0, 3] + received[0, 1]


def set_sums(first_vec, second_vec):
    product = (first_vec * second_vec).reshape(first_vec.shape[0], 2, 3, first_vec.shape[2])
    return jnp.sum(product, axis=(0, 2, 3))


def spread_sets(values):
    return jnp.repeat(values, 3)[None, :, None]


def butterfly_sum(values, axis):
    count = lax.axis_size(axis)
    stride = 1
    while stride < count:
        partner = lax.ppermute(values, axis, [(i, i ^ stride) for i in range(count)])
        values = values + partner
        stride *= 2
    return values


def global_sums(local_values):
    return butterfly_sum(butterfly_sum(local_values, "gx"), "gy")


def per_device(positions, polarity, direct_field, atom_count, pair_list, pair_count):
    blocks = positions.shape[2]
    atom_width = positions.shape[4]
    atom_mask = (
        jnp.arange(atom_width, dtype=jnp.int32)[None, :] < atom_count[0, 0][:, None]
    ).astype(jnp.float32)
    pol_wide = polarity[0, 0][:, None, :]
    geometry = jnp.concatenate([positions[0, 0], pol_wide], axis=1)
    entries = pair_list[0, 0]
    pair_total = pair_count[0, 0]
    presence = pair_presence(entries, pair_total, blocks)

    def mutual_field(geom_stack, dip_stack):
        own_total, other_acc = accumulate(geom_stack, dip_stack, presence)
        return (own_total + send_back(other_acc)) * atom_mask[:, None, :]

    residual = direct_field[0, 0] * atom_mask[:, None, :]
    search = pol_wide * residual
    stacked = neighbours(jnp.concatenate([geometry, search], axis=1))
    geom_stack = stacked[:, :, 0:4]
    dip_stack = stacked[:, :, 4:10]
    image = search / pol_wide - mutual_field(geom_stack, dip_stack)
    scaled = pol_wide * image
    scaled_dip = neighbours(scaled)
    image_scaled = scaled / pol_wide - mutual_field(geom_stack, scaled_dip)
    sums = global_sums(
        jnp.concatenate(
            [
                set_sums(residual, search),
                set_sums(search, image),
                set_sums(image, scaled),
                set_sums(search, image_scaled),
                set_sums(scaled, image_scaled),
            ]
        )
    )
    rho_now = sums[0:2]
    curv_now = sums[2:4]
    image_pre = sums[4:6]
    search_cross = sums[6:8]
    scaled_curv = sums[8:10]
    step_now = rho_now / curv_now
    step_size = spread_sets(step_now)
    dipoles = step_size * search
    residual = residual - step_size * image
    precond = pol_wide * residual
    precond_image = image - step_size * image_scaled
    rho_next = rho_now - 2.0 * step_now * curv_now + step_now * step_now * image_pre
    mixed = image_pre + search_cross
    precond_curv = curv_now - step_now * mixed + step_now * step_now * scaled_curv
    cross = 2.0 * curv_now - step_now * mixed
    ratio = rho_next / rho_now
    curv_next = precond_curv + ratio * cross + ratio * ratio * curv_now
    ratio_wide = spread_sets(ratio)
    search = precond + ratio_wide * search
    image = precond_image + ratio_wide * image
    step_size = spread_sets(rho_next / curv_next)
    dipoles = dipoles + step_size * search
    residual = residual - step_size * image
    return (dipoles[None, None], residual[None, None])


def solution(mesh):
    in_specs = (
        P("gx", "gy", None, None, None),
        P("gx", "gy", None, None),
        P("gx", "gy", None, None, None),
        P("gx", "gy", None),
        P("gx", "gy", None, None),
        P("gx", "gy"),
    )
    out_specs = (P("gx", "gy", None, None, None), P("gx", "gy", None, None, None))
    return jax.shard_map(
        per_device, mesh=mesh, in_specs=in_specs, out_specs=out_specs, check_vma=False
    )
```

```python
import jax
import jax.numpy as jnp
from jax import lax
from jax.sharding import PartitionSpec as P

ITERS = 2


thole_factor = 0.39
column_width = 8.0
slot_shift_x = (0.0, 0.0, 1.0, 1.0, 1.0)
slot_shift_y = (0.0, 1.0, -1.0, 0.0, 1.0)


def padded_2(cells, sides, width):
    for axis, dim in sides:
        count = lax.axis_size(axis)
        head = lax.slice_in_dim(cells, 0, width, axis=dim)
        tail = lax.slice_in_dim(cells, cells.shape[dim] - width, cells.shape[dim], axis=dim)
        cells = jnp.concatenate(
            [
                lax.ppermute(tail, axis, [(i, (i + 1) % count) for i in range(count)]),
                cells,
                lax.ppermute(head, axis, [((i + 1) % count, i) for i in range(count)]),
            ],
            axis=dim,
        )
    return cells


def from_behind(value, axis, steps):
    count = lax.axis_size(axis)
    pairs = [(source, (source + steps) % count) for source in range(count)]
    return lax.ppermute(value, axis, pairs)


def tensor_apply(coef_three, coef_five, deltas, moment, axis_sum):
    if axis_sum == 2:
        moments = [moment[:, member, None, :] for member in range(3)]
    else:
        moments = [moment[:, member, :, None] for member in range(3)]
    project = deltas[0] * moments[0] + deltas[1] * moments[1] + deltas[2] * moments[2]
    scaled = coef_five * project
    return jnp.stack(
        [
            jnp.sum(scaled * deltas[member] - coef_three * moments[member], axis=axis_sum)
            for member in range(3)
        ],
        axis=1,
    )


def pair_fields(geom_i, geom_j, dip_i, dip_j, slot_ids, same_block, two_way=True):
    chosen = (slot_ids[:, None] == jnp.arange(5, dtype=jnp.int32)[None, :]).astype(jnp.float32)
    offset_x = column_width * jnp.sum(
        chosen * jnp.array(slot_shift_x, jnp.float32)[None, :], axis=1
    )
    offset_y = column_width * jnp.sum(
        chosen * jnp.array(slot_shift_y, jnp.float32)[None, :], axis=1
    )
    delta_x = geom_j[:, 0, None, :] + offset_x[:, None, None] - geom_i[:, 0, :, None]
    delta_y = geom_j[:, 1, None, :] + offset_y[:, None, None] - geom_i[:, 1, :, None]
    delta_z = geom_j[:, 2, None, :] - geom_i[:, 2, :, None]
    dist_sq = delta_x * delta_x + delta_y * delta_y + delta_z * delta_z
    atom_width = geom_i.shape[2]
    same_atom = jnp.arange(atom_width)[:, None] == jnp.arange(atom_width)[None, :]
    diagonal = same_atom[None, :, :] & same_block[:, None, None]
    dist_sq = jnp.where(diagonal, 1.0, dist_sq)
    inv_dist = lax.rsqrt(dist_sq)
    inv_cube = inv_dist * inv_dist * inv_dist
    root_pol = jnp.sqrt(geom_i[:, 3, :, None] * geom_j[:, 3, None, :])
    damping = thole_factor * dist_sq * jnp.sqrt(dist_sq) / root_pol
    lambda_three = -jnp.expm1(-damping)
    lambda_five = lambda_three - damping * jnp.exp(-damping)
    keep_pair = jnp.where(diagonal, 0.0, 1.0)
    coef_three = keep_pair * lambda_three * inv_cube
    coef_five = keep_pair * 3.0 * lambda_five * inv_cube * inv_dist * inv_dist
    deltas = (delta_x, delta_y, delta_z)
    forward = jnp.concatenate(
        [
            tensor_apply(coef_three, coef_five, deltas, dip_j[:, 0:3], 2),
            tensor_apply(coef_three, coef_five, deltas, dip_j[:, 3:6], 2),
        ],
        axis=1,
    )
    if not two_way:
        return (forward, None)
    backward = jnp.concatenate(
        [
            tensor_apply(coef_three, coef_five, deltas, dip_i[:, 0:3], 1),
            tensor_apply(coef_three, coef_five, deltas, dip_i[:, 3:6], 1),
        ],
        axis=1,
    )
    return (forward, backward)


def pair_presence(entries, pair_total, blocks):
    live = jnp.arange(entries.shape[1], dtype=jnp.int32) < pair_total
    own_block, slot_ids, other_block = entries[0], entries[1], entries[2]
    shift = other_block - own_block + 1
    hit = (
        live[:, None, None, None]
        & (slot_ids[:, None, None, None] == jnp.arange(5, dtype=jnp.int32)[None, :, None, None])
        & (shift[:, None, None, None] == jnp.arange(3, dtype=jnp.int32)[None, None, :, None])
        & (own_block[:, None, None, None] == jnp.arange(blocks, dtype=jnp.int32)[None, None, None, :])
    )
    return jnp.sum(hit.astype(jnp.float32), axis=0)


def shifted_batch(own, other, blocks):
    first = jnp.concatenate([own[1:blocks], own, own[0 : blocks - 1]], axis=0)
    second = jnp.concatenate([other[0 : blocks - 1], other, other[1:blocks]], axis=0)
    return first, second


def gated(values, present):
    return jnp.where(present[:, None, None] > 0, values, 0.0)


def accumulate(geom_stack, dip_stack, presence):
    blocks = geom_stack.shape[1]
    geom_own = geom_stack[0]
    dip_own = dip_stack[0]
    same, _ = pair_fields(
        geom_own,
        geom_own,
        dip_own,
        dip_own,
        jnp.zeros((blocks,), jnp.int32),
        jnp.ones((blocks,), bool),
        two_way=False,
    )
    own_total = gated(same, presence[0, 1])
    count = blocks - 1
    forward, backward = pair_fields(
        geom_own[0:count],
        geom_own[1:blocks],
        dip_own[0:count],
        dip_own[1:blocks],
        jnp.zeros((count,), jnp.int32),
        jnp.zeros((count,), bool),
    )
    near = presence[0, 2, 0:count]
    zero_block = jnp.zeros_like(own_total[0:1])
    own_total = own_total + jnp.concatenate([gated(forward, near), zero_block], axis=0)
    own_total = own_total + jnp.concatenate([zero_block, gated(backward, near)], axis=0)
    own_i, _ = shifted_batch(geom_own, geom_own, blocks)
    dip_i, _ = shifted_batch(dip_own, dip_own, blocks)
    width = 3 * blocks - 2

    def one_slot(slot_index, carry):
        own_acc, other_acc = carry
        geom_j = lax.dynamic_index_in_dim(geom_stack, slot_index, 0, keepdims=False)
        dip_j = lax.dynamic_index_in_dim(dip_stack, slot_index, 0, keepdims=False)
        _, geom_j = shifted_batch(geom_j, geom_j, blocks)
        _, dip_j = shifted_batch(dip_j, dip_j, blocks)
        listed = lax.dynamic_index_in_dim(presence, slot_index, 0, keepdims=False)
        present = jnp.concatenate([listed[0, 1:blocks], listed[1], listed[2, 0:count]])
        forward, backward = pair_fields(
            own_i,
            geom_j,
            dip_i,
            dip_j,
            jnp.full((width,), slot_index, jnp.int32),
            jnp.zeros((width,), bool),
        )
        forward = gated(forward, present)
        backward = gated(backward, present)
        own_acc = (
            own_acc
            + jnp.concatenate([zero_block, forward[0:count]], axis=0)
            + forward[count : count + blocks]
            + jnp.concatenate([forward[count + blocks : width], zero_block], axis=0)
        )
        other_sum = (
            jnp.concatenate([backward[0:count], zero_block], axis=0)
            + backward[count : count + blocks]
            + jnp.concatenate([zero_block, backward[count + blocks : width]], axis=0)
        )
        other_acc = lax.dynamic_update_index_in_dim(other_acc, other_sum, slot_index - 1, 0)
        return own_acc, other_acc

    other_acc = jnp.zeros((4,) + own_total.shape, jnp.float32)
    return lax.fori_loop(1, 5, one_slot, (own_total, other_acc))


slot_moves = ((0, 1), (1, -1), (1, 0), (1, 1))


def shifted_from(value, move_x, move_y):
    count_x = lax.axis_size("gx")
    count_y = lax.axis_size("gy")
    if move_x == 0:
        pairs = [(source, (source - move_y) % count_y) for source in range(count_y)]
        return lax.ppermute(value, "gy", pairs)
    pairs = [
        (
            source_x * count_y + source_y,
            ((source_x - move_x) % count_x) * count_y + (source_y - move_y) % count_y,
        )
        for source_x in range(count_x)
        for source_y in range(count_y)
    ]
    return lax.ppermute(value, ("gx", "gy"), pairs)


def neighbours(block_data):
    gathered = [shifted_from(block_data, move_x, move_y) for move_x, move_y in slot_moves]
    return jnp.stack([block_data] + gathered, axis=0)


def send_back(partials):
    returned = [
        shifted_from(partials[index], -move_x, -move_y)
        for index, (move_x, move_y) in enumerate(slot_moves)
    ]
    return (returned[0] + returned[1]) + (returned[2] + returned[3])


def set_sums(first_vec, second_vec):
    product = (first_vec * second_vec).reshape(first_vec.shape[0], 2, 3, first_vec.shape[2])
    return jnp.sum(product, axis=(0, 2, 3))


def spread_sets(values):
    return jnp.repeat(values, 3)[None, :, None]


def butterfly_sum(values, axis):
    count = lax.axis_size(axis)
    stride = 1
    while stride < count:
        partner = lax.ppermute(values, axis, [(i, i ^ stride) for i in range(count)])
        values = values + partner
        stride *= 2
    return values


def global_sums(local_values):
    return butterfly_sum(butterfly_sum(local_values, "gx"), "gy")


def per_device(positions, polarity, direct_field, atom_count, pair_list, pair_count):
    blocks = positions.shape[2]
    atom_width = positions.shape[4]
    atom_mask = (
        jnp.arange(atom_width, dtype=jnp.int32)[None, :] < atom_count[0, 0][:, None]
    ).astype(jnp.float32)
    pol_wide = polarity[0, 0][:, None, :]
    geometry = jnp.concatenate([positions[0, 0], pol_wide], axis=1)
    entries = pair_list[0, 0]
    pair_total = pair_count[0, 0]
    presence = pair_presence(entries, pair_total, blocks)

    def mutual_field(geom_stack, dip_stack):
        own_total, other_acc = accumulate(geom_stack, dip_stack, presence)
        return (own_total + send_back(other_acc)) * atom_mask[:, None, :]

    residual = direct_field[0, 0] * atom_mask[:, None, :]
    search = pol_wide * residual
    stacked = neighbours(jnp.concatenate([geometry, search], axis=1))
    geom_stack = stacked[:, :, 0:4]
    dip_stack = stacked[:, :, 4:10]
    image = search / pol_wide - mutual_field(geom_stack, dip_stack)
    scaled = pol_wide * image
    scaled_dip = neighbours(scaled)
    image_scaled = scaled / pol_wide - mutual_field(geom_stack, scaled_dip)
    sums = global_sums(
        jnp.concatenate(
            [
                set_sums(residual, search),
                set_sums(search, image),
                set_sums(image, scaled),
                set_sums(search, image_scaled),
                set_sums(scaled, image_scaled),
            ]
        )
    )
    rho_now = sums[0:2]
    curv_now = sums[2:4]
    image_pre = sums[4:6]
    search_cross = sums[6:8]
    scaled_curv = sums[8:10]
    step_now = rho_now / curv_now
    step_size = spread_sets(step_now)
    dipoles = step_size * search
    residual = residual - step_size * image
    precond = pol_wide * residual
    precond_image = image - step_size * image_scaled
    rho_next = rho_now - 2.0 * step_now * curv_now + step_now * step_now * image_pre
    mixed = image_pre + search_cross
    precond_curv = curv_now - step_now * mixed + step_now * step_now * scaled_curv
    cross = 2.0 * curv_now - step_now * mixed
    ratio = rho_next / rho_now
    curv_next = precond_curv + ratio * cross + ratio * ratio * curv_now
    ratio_wide = spread_sets(ratio)
    search = precond + ratio_wide * search
    image = precond_image + ratio_wide * image
    step_size = spread_sets(rho_next / curv_next)
    dipoles = dipoles + step_size * search
    residual = residual - step_size * image
    return (dipoles[None, None], residual[None, None])


def solution(mesh):
    in_specs = (
        P("gx", "gy", None, None, None),
        P("gx", "gy", None, None),
        P("gx", "gy", None, None, None),
        P("gx", "gy", None),
        P("gx", "gy", None, None),
        P("gx", "gy"),
    )
    out_specs = (P("gx", "gy", None, None, None), P("gx", "gy", None, None, None))
    return jax.shard_map(
        per_device, mesh=mesh, in_specs=in_specs, out_specs=out_specs, check_vma=False
    )
```

```python
import jax
import jax.numpy as jnp
from jax import lax
from jax.sharding import PartitionSpec as P

ITERS = 2


thole_factor = 0.39
column_width = 8.0
slot_shift_x = (0.0, 0.0, 1.0, 1.0, 1.0)
slot_shift_y = (0.0, 1.0, -1.0, 0.0, 1.0)


def padded_2(cells, sides, width):
    for axis, dim in sides:
        count = lax.axis_size(axis)
        head = lax.slice_in_dim(cells, 0, width, axis=dim)
        tail = lax.slice_in_dim(cells, cells.shape[dim] - width, cells.shape[dim], axis=dim)
        cells = jnp.concatenate(
            [
                lax.ppermute(tail, axis, [(i, (i + 1) % count) for i in range(count)]),
                cells,
                lax.ppermute(head, axis, [((i + 1) % count, i) for i in range(count)]),
            ],
            axis=dim,
        )
    return cells


def from_behind(value, axis, steps):
    count = lax.axis_size(axis)
    pairs = [(source, (source + steps) % count) for source in range(count)]
    return lax.ppermute(value, axis, pairs)


def tensor_apply(coef_three, coef_five, deltas, moment, axis_sum):
    if axis_sum == 2:
        moments = [moment[:, member, None, :] for member in range(3)]
    else:
        moments = [moment[:, member, :, None] for member in range(3)]
    project = deltas[0] * moments[0] + deltas[1] * moments[1] + deltas[2] * moments[2]
    scaled = coef_five * project
    return jnp.stack(
        [
            jnp.sum(scaled * deltas[member] - coef_three * moments[member], axis=axis_sum)
            for member in range(3)
        ],
        axis=1,
    )


def pair_fields(geom_i, geom_j, dip_i, dip_j, slot_ids, same_block, two_way=True):
    chosen = (slot_ids[:, None] == jnp.arange(5, dtype=jnp.int32)[None, :]).astype(jnp.float32)
    offset_x = column_width * jnp.sum(
        chosen * jnp.array(slot_shift_x, jnp.float32)[None, :], axis=1
    )
    offset_y = column_width * jnp.sum(
        chosen * jnp.array(slot_shift_y, jnp.float32)[None, :], axis=1
    )
    delta_x = geom_j[:, 0, None, :] + offset_x[:, None, None] - geom_i[:, 0, :, None]
    delta_y = geom_j[:, 1, None, :] + offset_y[:, None, None] - geom_i[:, 1, :, None]
    delta_z = geom_j[:, 2, None, :] - geom_i[:, 2, :, None]
    dist_sq = delta_x * delta_x + delta_y * delta_y + delta_z * delta_z
    atom_width = geom_i.shape[2]
    same_atom = jnp.arange(atom_width)[:, None] == jnp.arange(atom_width)[None, :]
    diagonal = same_atom[None, :, :] & same_block[:, None, None]
    dist_sq = jnp.where(diagonal, 1.0, dist_sq)
    inv_dist = lax.rsqrt(dist_sq)
    inv_cube = inv_dist * inv_dist * inv_dist
    root_pol = jnp.sqrt(geom_i[:, 3, :, None] * geom_j[:, 3, None, :])
    damping = thole_factor * dist_sq * jnp.sqrt(dist_sq) / root_pol
    lambda_three = -jnp.expm1(-damping)
    lambda_five = lambda_three - damping * jnp.exp(-damping)
    keep_pair = jnp.where(diagonal, 0.0, 1.0)
    coef_three = keep_pair * lambda_three * inv_cube
    coef_five = keep_pair * 3.0 * lambda_five * inv_cube * inv_dist * inv_dist
    deltas = (delta_x, delta_y, delta_z)
    forward = jnp.concatenate(
        [
            tensor_apply(coef_three, coef_five, deltas, dip_j[:, 0:3], 2),
            tensor_apply(coef_three, coef_five, deltas, dip_j[:, 3:6], 2),
        ],
        axis=1,
    )
    if not two_way:
        return (forward, None)
    backward = jnp.concatenate(
        [
            tensor_apply(coef_three, coef_five, deltas, dip_i[:, 0:3], 1),
            tensor_apply(coef_three, coef_five, deltas, dip_i[:, 3:6], 1),
        ],
        axis=1,
    )
    return (forward, backward)


def pair_presence(entries, pair_total, blocks):
    live = jnp.arange(entries.shape[1], dtype=jnp.int32) < pair_total
    own_block, slot_ids, other_block = entries[0], entries[1], entries[2]
    shift = other_block - own_block + 1
    hit = (
        live[:, None, None, None]
        & (slot_ids[:, None, None, None] == jnp.arange(5, dtype=jnp.int32)[None, :, None, None])
        & (shift[:, None, None, None] == jnp.arange(3, dtype=jnp.int32)[None, None, :, None])
        & (own_block[:, None, None, None] == jnp.arange(blocks, dtype=jnp.int32)[None, None, None, :])
    )
    return jnp.sum(hit.astype(jnp.float32), axis=0)


def shifted_batch(own, other, blocks):
    first = jnp.concatenate([own[1:blocks], own, own[0 : blocks - 1]], axis=0)
    second = jnp.concatenate([other[0 : blocks - 1], other, other[1:blocks]], axis=0)
    return first, second


def gated(values, present):
    return jnp.where(present[:, None, None] > 0, values, 0.0)


def accumulate(geom_stack, dip_stack, presence):
    blocks = geom_stack.shape[1]
    geom_own = geom_stack[0]
    dip_own = dip_stack[0]
    same, _ = pair_fields(
        geom_own,
        geom_own,
        dip_own,
        dip_own,
        jnp.zeros((blocks,), jnp.int32),
        jnp.ones((blocks,), bool),
        two_way=False,
    )
    own_total = gated(same, presence[0, 1])
    count = blocks - 1
    forward, backward = pair_fields(
        geom_own[0:count],
        geom_own[1:blocks],
        dip_own[0:count],
        dip_own[1:blocks],
        jnp.zeros((count,), jnp.int32),
        jnp.zeros((count,), bool),
    )
    near = presence[0, 2, 0:count]
    zero_block = jnp.zeros_like(own_total[0:1])
    own_total = own_total + jnp.concatenate([gated(forward, near), zero_block], axis=0)
    own_total = own_total + jnp.concatenate([zero_block, gated(backward, near)], axis=0)
    own_i, _ = shifted_batch(geom_own, geom_own, blocks)
    dip_i, _ = shifted_batch(dip_own, dip_own, blocks)
    width = 3 * blocks - 2

    def one_slot(slot_index, carry):
        own_acc, other_acc = carry
        geom_j = lax.dynamic_index_in_dim(geom_stack, slot_index, 0, keepdims=False)
        dip_j = lax.dynamic_index_in_dim(dip_stack, slot_index, 0, keepdims=False)
        _, geom_j = shifted_batch(geom_j, geom_j, blocks)
        _, dip_j = shifted_batch(dip_j, dip_j, blocks)
        listed = lax.dynamic_index_in_dim(presence, slot_index, 0, keepdims=False)
        present = jnp.concatenate([listed[0, 1:blocks], listed[1], listed[2, 0:count]])
        forward, backward = pair_fields(
            own_i,
            geom_j,
            dip_i,
            dip_j,
            jnp.full((width,), slot_index, jnp.int32),
            jnp.zeros((width,), bool),
        )
        forward = gated(forward, present)
        backward = gated(backward, present)
        own_acc = (
            own_acc
            + jnp.concatenate([zero_block, forward[0:count]], axis=0)
            + forward[count : count + blocks]
            + jnp.concatenate([forward[count + blocks : width], zero_block], axis=0)
        )
        other_sum = (
            jnp.concatenate([backward[0:count], zero_block], axis=0)
            + backward[count : count + blocks]
            + jnp.concatenate([zero_block, backward[count + blocks : width]], axis=0)
        )
        other_acc = lax.dynamic_update_index_in_dim(other_acc, other_sum, slot_index - 1, 0)
        return own_acc, other_acc

    other_acc = jnp.zeros((4,) + own_total.shape, jnp.float32)
    return lax.fori_loop(1, 5, one_slot, (own_total, other_acc))


def neighbours(block_data):
    column = padded_2(block_data[None, None], (("gy", 1),), 1)
    across = from_behind(column, "gx", -1)
    return jnp.concatenate([block_data[None], column[0, 2:3], across[0]], axis=0)


def send_back(partials):
    received = from_behind(partials[None, 1:4], "gx", 1)
    paired = jnp.stack([received[0, 0], received[0, 2] + partials[0]], axis=0)[None]
    column = padded_2(paired, (("gy", 1),), 1)
    return column[0, 0] + column[0, 3] + received[0, 1]


def set_sums(first_vec, second_vec):
    product = (first_vec * second_vec).reshape(first_vec.shape[0], 2, 3, first_vec.shape[2])
    return jnp.sum(product, axis=(0, 2, 3))


def spread_sets(values):
    return jnp.repeat(values, 3)[None, :, None]


def butterfly_sum(values, axis):
    count = lax.axis_size(axis)
    stride = 1
    while stride < count:
        partner = lax.ppermute(values, axis, [(i, i ^ stride) for i in range(count)])
        values = values + partner
        stride *= 2
    return values


def field_dot(values, own_total, other_acc):
    total = set_sums(values[0], own_total)
    for slot_index in range(other_acc.shape[0]):
        total = total + set_sums(values[slot_index + 1], other_acc[slot_index])
    return total


def global_sums(local_values):
    return butterfly_sum(butterfly_sum(local_values, "gx"), "gy")


def per_device(positions, polarity, direct_field, atom_count, pair_list, pair_count):
    blocks = positions.shape[2]
    atom_width = positions.shape[4]
    atom_mask = (
        jnp.arange(atom_width, dtype=jnp.int32)[None, :] < atom_count[0, 0][:, None]
    ).astype(jnp.float32)
    pol_wide = polarity[0, 0][:, None, :]
    geometry = jnp.concatenate([positions[0, 0], pol_wide], axis=1)
    entries = pair_list[0, 0]
    pair_total = pair_count[0, 0]
    presence = pair_presence(entries, pair_total, blocks)

    def mutual_field(geom_stack, dip_stack):
        own_total, other_acc = accumulate(geom_stack, dip_stack, presence)
        return (own_total + send_back(other_acc)) * atom_mask[:, None, :]

    residual = direct_field[0, 0] * atom_mask[:, None, :]
    search = pol_wide * residual
    stacked = neighbours(jnp.concatenate([geometry, search], axis=1))
    geom_stack = stacked[:, :, 0:4]
    dip_stack = stacked[:, :, 4:10]
    image = search / pol_wide - mutual_field(geom_stack, dip_stack)
    scaled = pol_wide * image
    scaled_dip = neighbours(scaled)
    own_second, other_second = accumulate(geom_stack, scaled_dip, presence)
    search_field = field_dot(dip_stack, own_second, other_second)
    scaled_field = field_dot(scaled_dip, own_second, other_second)
    image_scaled = scaled / pol_wide - (own_second + send_back(other_second)) * atom_mask[:, None, :]
    sums = global_sums(
        jnp.concatenate(
            [
                set_sums(residual, search),
                set_sums(search, image),
                set_sums(image, scaled),
                set_sums(search, scaled / pol_wide) - search_field,
                set_sums(scaled, scaled / pol_wide) - scaled_field,
            ]
        )
    )
    rho_now = sums[0:2]
    curv_now = sums[2:4]
    image_pre = sums[4:6]
    search_cross = sums[6:8]
    scaled_curv = sums[8:10]
    step_now = rho_now / curv_now
    step_size = spread_sets(step_now)
    dipoles = step_size * search
    residual = residual - step_size * image
    precond = pol_wide * residual
    precond_image = image - step_size * image_scaled
    rho_next = rho_now - 2.0 * step_now * curv_now + step_now * step_now * image_pre
    mixed = image_pre + search_cross
    precond_curv = curv_now - step_now * mixed + step_now * step_now * scaled_curv
    cross = 2.0 * curv_now - step_now * mixed
    ratio = rho_next / rho_now
    curv_next = precond_curv + ratio * cross + ratio * ratio * curv_now
    ratio_wide = spread_sets(ratio)
    search = precond + ratio_wide * search
    image = precond_image + ratio_wide * image
    step_size = spread_sets(rho_next / curv_next)
    dipoles = dipoles + step_size * search
    residual = residual - step_size * image
    return (dipoles[None, None], residual[None, None])


def solution(mesh):
    in_specs = (
        P("gx", "gy", None, None, None),
        P("gx", "gy", None, None),
        P("gx", "gy", None, None, None),
        P("gx", "gy", None),
        P("gx", "gy", None, None),
        P("gx", "gy"),
    )
    out_specs = (P("gx", "gy", None, None, None), P("gx", "gy", None, None, None))
    return jax.shard_map(
        per_device, mesh=mesh, in_specs=in_specs, out_specs=out_specs, check_vma=False
    )
```

```python
import jax
import jax.numpy as jnp
from jax import lax
from jax.sharding import PartitionSpec as P

ITERS = 2


thole_factor = 0.39
column_width = 8.0
slot_shift_x = (0.0, 0.0, 1.0, 1.0, 1.0)
slot_shift_y = (0.0, 1.0, -1.0, 0.0, 1.0)


def padded_2(cells, sides, width):
    for axis, dim in sides:
        count = lax.axis_size(axis)
        head = lax.slice_in_dim(cells, 0, width, axis=dim)
        tail = lax.slice_in_dim(cells, cells.shape[dim] - width, cells.shape[dim], axis=dim)
        cells = jnp.concatenate(
            [
                lax.ppermute(tail, axis, [(i, (i + 1) % count) for i in range(count)]),
                cells,
                lax.ppermute(head, axis, [((i + 1) % count, i) for i in range(count)]),
            ],
            axis=dim,
        )
    return cells


def from_behind(value, axis, steps):
    count = lax.axis_size(axis)
    pairs = [(source, (source + steps) % count) for source in range(count)]
    return lax.ppermute(value, axis, pairs)


def tensor_apply(coef_three, coef_five, deltas, moment, axis_sum):
    if axis_sum == 2:
        moments = [moment[:, member, None, :] for member in range(3)]
    else:
        moments = [moment[:, member, :, None] for member in range(3)]
    project = deltas[0] * moments[0] + deltas[1] * moments[1] + deltas[2] * moments[2]
    scaled = coef_five * project
    return jnp.stack(
        [
            jnp.sum(scaled * deltas[member] - coef_three * moments[member], axis=axis_sum)
            for member in range(3)
        ],
        axis=1,
    )


def pair_fields(geom_i, geom_j, dip_i, dip_j, slot_ids, same_block, two_way=True):
    chosen = (slot_ids[:, None] == jnp.arange(5, dtype=jnp.int32)[None, :]).astype(jnp.float32)
    offset_x = column_width * jnp.sum(
        chosen * jnp.array(slot_shift_x, jnp.float32)[None, :], axis=1
    )
    offset_y = column_width * jnp.sum(
        chosen * jnp.array(slot_shift_y, jnp.float32)[None, :], axis=1
    )
    delta_x = geom_j[:, 0, None, :] + offset_x[:, None, None] - geom_i[:, 0, :, None]
    delta_y = geom_j[:, 1, None, :] + offset_y[:, None, None] - geom_i[:, 1, :, None]
    delta_z = geom_j[:, 2, None, :] - geom_i[:, 2, :, None]
    dist_sq = delta_x * delta_x + delta_y * delta_y + delta_z * delta_z
    atom_width = geom_i.shape[2]
    same_atom = jnp.arange(atom_width)[:, None] == jnp.arange(atom_width)[None, :]
    diagonal = same_atom[None, :, :] & same_block[:, None, None]
    dist_sq = jnp.where(diagonal, 1.0, dist_sq)
    inv_dist = lax.rsqrt(dist_sq)
    inv_cube = inv_dist * inv_dist * inv_dist
    root_pol = jnp.sqrt(geom_i[:, 3, :, None] * geom_j[:, 3, None, :])
    damping = thole_factor * dist_sq * jnp.sqrt(dist_sq) / root_pol
    lambda_three = -jnp.expm1(-damping)
    lambda_five = lambda_three - damping * jnp.exp(-damping)
    keep_pair = jnp.where(diagonal, 0.0, 1.0)
    coef_three = keep_pair * lambda_three * inv_cube
    coef_five = keep_pair * 3.0 * lambda_five * inv_cube * inv_dist * inv_dist
    deltas = (delta_x, delta_y, delta_z)
    forward = jnp.concatenate(
        [
            tensor_apply(coef_three, coef_five, deltas, dip_j[:, 0:3], 2),
            tensor_apply(coef_three, coef_five, deltas, dip_j[:, 3:6], 2),
        ],
        axis=1,
    )
    if not two_way:
        return (forward, None)
    backward = jnp.concatenate(
        [
            tensor_apply(coef_three, coef_five, deltas, dip_i[:, 0:3], 1),
            tensor_apply(coef_three, coef_five, deltas, dip_i[:, 3:6], 1),
        ],
        axis=1,
    )
    return (forward, backward)


def pair_presence(entries, pair_total, blocks):
    live = jnp.arange(entries.shape[1], dtype=jnp.int32) < pair_total
    own_block, slot_ids, other_block = entries[0], entries[1], entries[2]
    shift = other_block - own_block + 1
    hit = (
        live[:, None, None, None]
        & (slot_ids[:, None, None, None] == jnp.arange(5, dtype=jnp.int32)[None, :, None, None])
        & (shift[:, None, None, None] == jnp.arange(3, dtype=jnp.int32)[None, None, :, None])
        & (own_block[:, None, None, None] == jnp.arange(blocks, dtype=jnp.int32)[None, None, None, :])
    )
    return jnp.sum(hit.astype(jnp.float32), axis=0)


def shifted_batch(own, other, blocks):
    first = jnp.concatenate([own[1:blocks], own, own[0 : blocks - 1]], axis=0)
    second = jnp.concatenate([other[0 : blocks - 1], other, other[1:blocks]], axis=0)
    return first, second


def gated(values, present):
    return jnp.where(present[:, None, None] > 0, values, 0.0)


def accumulate(geom_stack, dip_stack, presence):
    blocks = geom_stack.shape[1]
    geom_own = geom_stack[0]
    dip_own = dip_stack[0]
    same, _ = pair_fields(
        geom_own,
        geom_own,
        dip_own,
        dip_own,
        jnp.zeros((blocks,), jnp.int32),
        jnp.ones((blocks,), bool),
        two_way=False,
    )
    own_total = gated(same, presence[0, 1])
    count = blocks - 1
    forward, backward = pair_fields(
        geom_own[0:count],
        geom_own[1:blocks],
        dip_own[0:count],
        dip_own[1:blocks],
        jnp.zeros((count,), jnp.int32),
        jnp.zeros((count,), bool),
    )
    near = presence[0, 2, 0:count]
    zero_block = jnp.zeros_like(own_total[0:1])
    own_total = own_total + jnp.concatenate([gated(forward, near), zero_block], axis=0)
    own_total = own_total + jnp.concatenate([zero_block, gated(backward, near)], axis=0)
    own_i, _ = shifted_batch(geom_own, geom_own, blocks)
    dip_i, _ = shifted_batch(dip_own, dip_own, blocks)
    width = 3 * blocks - 2

    def one_slot(slot_index, carry):
        own_acc, other_acc = carry
        geom_j = lax.dynamic_index_in_dim(geom_stack, slot_index, 0, keepdims=False)
        dip_j = lax.dynamic_index_in_dim(dip_stack, slot_index, 0, keepdims=False)
        _, geom_j = shifted_batch(geom_j, geom_j, blocks)
        _, dip_j = shifted_batch(dip_j, dip_j, blocks)
        listed = lax.dynamic_index_in_dim(presence, slot_index, 0, keepdims=False)
        present = jnp.concatenate([listed[0, 1:blocks], listed[1], listed[2, 0:count]])
        forward, backward = pair_fields(
            own_i,
            geom_j,
            dip_i,
            dip_j,
            jnp.full((width,), slot_index, jnp.int32),
            jnp.zeros((width,), bool),
        )
        forward = gated(forward, present)
        backward = gated(backward, present)
        own_acc = (
            own_acc
            + jnp.concatenate([zero_block, forward[0:count]], axis=0)
            + forward[count : count + blocks]
            + jnp.concatenate([forward[count + blocks : width], zero_block], axis=0)
        )
        other_sum = (
            jnp.concatenate([backward[0:count], zero_block], axis=0)
            + backward[count : count + blocks]
            + jnp.concatenate([zero_block, backward[count + blocks : width]], axis=0)
        )
        other_acc = lax.dynamic_update_index_in_dim(other_acc, other_sum, slot_index - 1, 0)
        return own_acc, other_acc

    other_acc = jnp.zeros((4,) + own_total.shape, jnp.float32)
    return lax.fori_loop(1, 5, one_slot, (own_total, other_acc))


def neighbours(block_data):
    column = padded_2(block_data[None, None], (("gy", 1),), 1)
    across = from_behind(column, "gx", -1)
    return jnp.concatenate([block_data[None], column[0, 2:3], across[0]], axis=0)


def send_back(partials):
    received = from_behind(partials[None, 1:4], "gx", 1)
    paired = jnp.stack([received[0, 0], received[0, 2] + partials[0]], axis=0)[None]
    column = padded_2(paired, (("gy", 1),), 1)
    return column[0, 0] + column[0, 3] + received[0, 1]


def set_sums(first_vec, second_vec):
    product = (first_vec * second_vec).reshape(first_vec.shape[0], 2, 3, first_vec.shape[2])
    return jnp.sum(product, axis=(0, 2, 3))


def spread_sets(values):
    return jnp.repeat(values, 3)[None, :, None]


def butterfly_sum(values, axis, first=1, last=None):
    count = lax.axis_size(axis)
    bound = count if last is None else min(last, count)
    stride = first
    while stride < bound:
        partner = lax.ppermute(values, axis, [(i, i ^ stride) for i in range(count)])
        values = values + partner
        stride *= 2
    return values


def field_dot(values, own_total, other_acc):
    total = set_sums(values[0], own_total)
    for slot_index in range(other_acc.shape[0]):
        total = total + set_sums(values[slot_index + 1], other_acc[slot_index])
    return total


def global_sums(local_values):
    return butterfly_sum(butterfly_sum(local_values, "gx"), "gy")


def per_device(positions, polarity, direct_field, atom_count, pair_list, pair_count):
    blocks = positions.shape[2]
    atom_width = positions.shape[4]
    atom_mask = (
        jnp.arange(atom_width, dtype=jnp.int32)[None, :] < atom_count[0, 0][:, None]
    ).astype(jnp.float32)
    pol_wide = polarity[0, 0][:, None, :]
    geometry = jnp.concatenate([positions[0, 0], pol_wide], axis=1)
    entries = pair_list[0, 0]
    pair_total = pair_count[0, 0]
    presence = pair_presence(entries, pair_total, blocks)

    def mutual_field(geom_stack, dip_stack):
        own_total, other_acc = accumulate(geom_stack, dip_stack, presence)
        return (own_total + send_back(other_acc)) * atom_mask[:, None, :]

    residual = direct_field[0, 0] * atom_mask[:, None, :]
    search = pol_wide * residual
    stacked = neighbours(jnp.concatenate([geometry, search], axis=1))
    geom_stack = stacked[:, :, 0:4]
    dip_stack = stacked[:, :, 4:10]
    image = search / pol_wide - mutual_field(geom_stack, dip_stack)
    scaled = pol_wide * image
    scaled_dip = neighbours(scaled)
    own_second, other_second = accumulate(geom_stack, scaled_dip, presence)
    search_field = field_dot(dip_stack, own_second, other_second)
    scaled_field = field_dot(scaled_dip, own_second, other_second)
    sums = butterfly_sum(
        jnp.concatenate(
            [
                set_sums(residual, search),
                set_sums(search, image),
                set_sums(image, scaled),
                set_sums(search, scaled / pol_wide) - search_field,
                set_sums(scaled, scaled / pol_wide) - scaled_field,
            ]
        ),
        "gx",
    )
    sums, other_second = lax.optimization_barrier((sums, other_second))
    received = from_behind(other_second[None, 1:4], "gx", 1)
    sums = butterfly_sum(sums, "gy", last=4)
    sums, received = lax.optimization_barrier((sums, received))
    paired = jnp.stack([received[0, 0], received[0, 2] + other_second[0]], axis=0)[None]
    column = padded_2(paired, (("gy", 1),), 1)
    sums = butterfly_sum(sums, "gy", first=4)
    returned = column[0, 0] + column[0, 3] + received[0, 1]
    image_scaled = scaled / pol_wide - (own_second + returned) * atom_mask[:, None, :]
    rho_now = sums[0:2]
    curv_now = sums[2:4]
    image_pre = sums[4:6]
    search_cross = sums[6:8]
    scaled_curv = sums[8:10]
    step_now = rho_now / curv_now
    step_size = spread_sets(step_now)
    dipoles = step_size * search
    residual = residual - step_size * image
    precond = pol_wide * residual
    precond_image = image - step_size * image_scaled
    rho_next = rho_now - 2.0 * step_now * curv_now + step_now * step_now * image_pre
    mixed = image_pre + search_cross
    precond_curv = curv_now - step_now * mixed + step_now * step_now * scaled_curv
    cross = 2.0 * curv_now - step_now * mixed
    ratio = rho_next / rho_now
    curv_next = precond_curv + ratio * cross + ratio * ratio * curv_now
    ratio_wide = spread_sets(ratio)
    search = precond + ratio_wide * search
    image = precond_image + ratio_wide * image
    step_size = spread_sets(rho_next / curv_next)
    dipoles = dipoles + step_size * search
    residual = residual - step_size * image
    return (dipoles[None, None], residual[None, None])


def solution(mesh):
    in_specs = (
        P("gx", "gy", None, None, None),
        P("gx", "gy", None, None),
        P("gx", "gy", None, None, None),
        P("gx", "gy", None),
        P("gx", "gy", None, None),
        P("gx", "gy"),
    )
    out_specs = (P("gx", "gy", None, None, None), P("gx", "gy", None, None, None))
    return jax.shard_map(
        per_device, mesh=mesh, in_specs=in_specs, out_specs=out_specs, check_vma=False
    )
```

```python
import jax
import jax.numpy as jnp
from jax import lax
from jax.sharding import PartitionSpec as P

ITERS = 2


thole_factor = 0.39
column_width = 8.0
slot_shift_x = (0.0, 0.0, 1.0, 1.0, 1.0)
slot_shift_y = (0.0, 1.0, -1.0, 0.0, 1.0)


def padded_2(cells, sides, width):
    for axis, dim in sides:
        count = lax.axis_size(axis)
        head = lax.slice_in_dim(cells, 0, width, axis=dim)
        tail = lax.slice_in_dim(cells, cells.shape[dim] - width, cells.shape[dim], axis=dim)
        cells = jnp.concatenate(
            [
                lax.ppermute(tail, axis, [(i, (i + 1) % count) for i in range(count)]),
                cells,
                lax.ppermute(head, axis, [((i + 1) % count, i) for i in range(count)]),
            ],
            axis=dim,
        )
    return cells


def from_behind(value, axis, steps):
    count = lax.axis_size(axis)
    pairs = [(source, (source + steps) % count) for source in range(count)]
    return lax.ppermute(value, axis, pairs)


def tensor_apply(coef_three, coef_five, deltas, moment, axis_sum):
    if axis_sum == 2:
        moments = [moment[:, member, None, :] for member in range(3)]
    else:
        moments = [moment[:, member, :, None] for member in range(3)]
    project = deltas[0] * moments[0] + deltas[1] * moments[1] + deltas[2] * moments[2]
    scaled = coef_five * project
    return jnp.stack(
        [
            jnp.sum(scaled * deltas[member] - coef_three * moments[member], axis=axis_sum)
            for member in range(3)
        ],
        axis=1,
    )


def pair_fields(geom_i, geom_j, dip_i, dip_j, slot_ids, same_block, two_way=True):
    chosen = (slot_ids[:, None] == jnp.arange(5, dtype=jnp.int32)[None, :]).astype(jnp.float32)
    offset_x = column_width * jnp.sum(
        chosen * jnp.array(slot_shift_x, jnp.float32)[None, :], axis=1
    )
    offset_y = column_width * jnp.sum(
        chosen * jnp.array(slot_shift_y, jnp.float32)[None, :], axis=1
    )
    delta_x = geom_j[:, 0, None, :] + offset_x[:, None, None] - geom_i[:, 0, :, None]
    delta_y = geom_j[:, 1, None, :] + offset_y[:, None, None] - geom_i[:, 1, :, None]
    delta_z = geom_j[:, 2, None, :] - geom_i[:, 2, :, None]
    dist_sq = delta_x * delta_x + delta_y * delta_y + delta_z * delta_z
    atom_width = geom_i.shape[2]
    same_atom = jnp.arange(atom_width)[:, None] == jnp.arange(atom_width)[None, :]
    diagonal = same_atom[None, :, :] & same_block[:, None, None]
    dist_sq = jnp.where(diagonal, 1.0, dist_sq)
    inv_dist = lax.rsqrt(dist_sq)
    inv_cube = inv_dist * inv_dist * inv_dist
    root_pol = jnp.sqrt(geom_i[:, 3, :, None] * geom_j[:, 3, None, :])
    damping = thole_factor * dist_sq * jnp.sqrt(dist_sq) / root_pol
    lambda_three = -jnp.expm1(-damping)
    lambda_five = lambda_three - damping * jnp.exp(-damping)
    keep_pair = jnp.where(diagonal, 0.0, 1.0)
    coef_three = keep_pair * lambda_three * inv_cube
    coef_five = keep_pair * 3.0 * lambda_five * inv_cube * inv_dist * inv_dist
    deltas = (delta_x, delta_y, delta_z)
    forward = jnp.concatenate(
        [
            tensor_apply(coef_three, coef_five, deltas, dip_j[:, 0:3], 2),
            tensor_apply(coef_three, coef_five, deltas, dip_j[:, 3:6], 2),
        ],
        axis=1,
    )
    if not two_way:
        return (forward, None)
    backward = jnp.concatenate(
        [
            tensor_apply(coef_three, coef_five, deltas, dip_i[:, 0:3], 1),
            tensor_apply(coef_three, coef_five, deltas, dip_i[:, 3:6], 1),
        ],
        axis=1,
    )
    return (forward, backward)


def pair_presence(entries, pair_total, blocks):
    live = jnp.arange(entries.shape[1], dtype=jnp.int32) < pair_total
    own_block, slot_ids, other_block = entries[0], entries[1], entries[2]
    shift = other_block - own_block + 1
    hit = (
        live[:, None, None, None]
        & (slot_ids[:, None, None, None] == jnp.arange(5, dtype=jnp.int32)[None, :, None, None])
        & (shift[:, None, None, None] == jnp.arange(3, dtype=jnp.int32)[None, None, :, None])
        & (own_block[:, None, None, None] == jnp.arange(blocks, dtype=jnp.int32)[None, None, None, :])
    )
    return jnp.sum(hit.astype(jnp.float32), axis=0)


def shifted_batch(own, other, blocks):
    first = jnp.concatenate([own[1:blocks], own, own[0 : blocks - 1]], axis=0)
    second = jnp.concatenate([other[0 : blocks - 1], other, other[1:blocks]], axis=0)
    return first, second


def gated(values, present):
    return jnp.where(present[:, None, None] > 0, values, 0.0)


def accumulate(geom_stack, dip_stack, presence):
    blocks = geom_stack.shape[1]
    geom_own = geom_stack[0]
    dip_own = dip_stack[0]
    same, _ = pair_fields(
        geom_own,
        geom_own,
        dip_own,
        dip_own,
        jnp.zeros((blocks,), jnp.int32),
        jnp.ones((blocks,), bool),
        two_way=False,
    )
    own_total = gated(same, presence[0, 1])
    count = blocks - 1
    forward, backward = pair_fields(
        geom_own[0:count],
        geom_own[1:blocks],
        dip_own[0:count],
        dip_own[1:blocks],
        jnp.zeros((count,), jnp.int32),
        jnp.zeros((count,), bool),
    )
    near = presence[0, 2, 0:count]
    zero_block = jnp.zeros_like(own_total[0:1])
    own_total = own_total + jnp.concatenate([gated(forward, near), zero_block], axis=0)
    own_total = own_total + jnp.concatenate([zero_block, gated(backward, near)], axis=0)
    own_i, _ = shifted_batch(geom_own, geom_own, blocks)
    dip_i, _ = shifted_batch(dip_own, dip_own, blocks)
    width = 3 * blocks - 2

    def one_slot(slot_index, carry):
        own_acc, other_acc = carry
        geom_j = lax.dynamic_index_in_dim(geom_stack, slot_index, 0, keepdims=False)
        dip_j = lax.dynamic_index_in_dim(dip_stack, slot_index, 0, keepdims=False)
        _, geom_j = shifted_batch(geom_j, geom_j, blocks)
        _, dip_j = shifted_batch(dip_j, dip_j, blocks)
        listed = lax.dynamic_index_in_dim(presence, slot_index, 0, keepdims=False)
        present = jnp.concatenate([listed[0, 1:blocks], listed[1], listed[2, 0:count]])
        forward, backward = pair_fields(
            own_i,
            geom_j,
            dip_i,
            dip_j,
            jnp.full((width,), slot_index, jnp.int32),
            jnp.zeros((width,), bool),
        )
        forward = gated(forward, present)
        backward = gated(backward, present)
        own_acc = (
            own_acc
            + jnp.concatenate([zero_block, forward[0:count]], axis=0)
            + forward[count : count + blocks]
            + jnp.concatenate([forward[count + blocks : width], zero_block], axis=0)
        )
        other_sum = (
            jnp.concatenate([backward[0:count], zero_block], axis=0)
            + backward[count : count + blocks]
            + jnp.concatenate([zero_block, backward[count + blocks : width]], axis=0)
        )
        other_acc = lax.dynamic_update_index_in_dim(other_acc, other_sum, slot_index - 1, 0)
        return own_acc, other_acc

    other_acc = jnp.zeros((4,) + own_total.shape, jnp.float32)
    carry = one_slot(1, (own_total, other_acc))
    return lax.fori_loop(2, 5, one_slot, carry)


def neighbours(block_data):
    column = padded_2(block_data[None, None], (("gy", 1),), 1)
    across = from_behind(column, "gx", -1)
    return jnp.concatenate([block_data[None], column[0, 2:3], across[0]], axis=0)


def send_back(partials):
    received = from_behind(partials[None, 1:4], "gx", 1)
    paired = jnp.stack([received[0, 0], received[0, 2] + partials[0]], axis=0)[None]
    column = padded_2(paired, (("gy", 1),), 1)
    return column[0, 0] + column[0, 3] + received[0, 1]


def set_sums(first_vec, second_vec):
    product = (first_vec * second_vec).reshape(first_vec.shape[0], 2, 3, first_vec.shape[2])
    return jnp.sum(product, axis=(0, 2, 3))


def spread_sets(values):
    return jnp.repeat(values, 3)[None, :, None]


def butterfly_sum(values, axis, first=1, last=None):
    count = lax.axis_size(axis)
    bound = count if last is None else min(last, count)
    stride = first
    while stride < bound:
        partner = lax.ppermute(values, axis, [(i, i ^ stride) for i in range(count)])
        values = values + partner
        stride *= 2
    return values


def field_dot(values, own_total, other_acc):
    total = set_sums(values[0], own_total)
    for slot_index in range(other_acc.shape[0]):
        total = total + set_sums(values[slot_index + 1], other_acc[slot_index])
    return total


def global_sums(local_values):
    return butterfly_sum(butterfly_sum(local_values, "gx"), "gy")


def per_device(positions, polarity, direct_field, atom_count, pair_list, pair_count):
    blocks = positions.shape[2]
    atom_width = positions.shape[4]
    atom_mask = (
        jnp.arange(atom_width, dtype=jnp.int32)[None, :] < atom_count[0, 0][:, None]
    ).astype(jnp.float32)
    pol_wide = polarity[0, 0][:, None, :]
    geometry = jnp.concatenate([positions[0, 0], pol_wide], axis=1)
    entries = pair_list[0, 0]
    pair_total = pair_count[0, 0]
    presence = pair_presence(entries, pair_total, blocks)

    def mutual_field(geom_stack, dip_stack):
        own_total, other_acc = accumulate(geom_stack, dip_stack, presence)
        return (own_total + send_back(other_acc)) * atom_mask[:, None, :]

    residual = direct_field[0, 0] * atom_mask[:, None, :]
    search = pol_wide * residual
    stacked = neighbours(jnp.concatenate([geometry, search], axis=1))
    geom_stack = stacked[:, :, 0:4]
    dip_stack = stacked[:, :, 4:10]
    image = search / pol_wide - mutual_field(geom_stack, dip_stack)
    scaled = pol_wide * image
    scaled_dip = neighbours(scaled)
    own_second, other_second = accumulate(geom_stack, scaled_dip, presence)
    search_field = field_dot(dip_stack, own_second, other_second)
    scaled_field = field_dot(scaled_dip, own_second, other_second)
    sums = butterfly_sum(
        jnp.concatenate(
            [
                set_sums(residual, search),
                set_sums(search, image),
                set_sums(image, scaled),
                set_sums(search, scaled / pol_wide) - search_field,
                set_sums(scaled, scaled / pol_wide) - scaled_field,
            ]
        ),
        "gx",
    )
    sums, other_second = lax.optimization_barrier((sums, other_second))
    received = from_behind(other_second[None, 1:4], "gx", 1)
    sums = butterfly_sum(sums, "gy", last=4)
    sums, received = lax.optimization_barrier((sums, received))
    paired = jnp.stack([received[0, 0], received[0, 2] + other_second[0]], axis=0)[None]
    column = padded_2(paired, (("gy", 1),), 1)
    sums = butterfly_sum(sums, "gy", first=4)
    returned = column[0, 0] + column[0, 3] + received[0, 1]
    image_scaled = scaled / pol_wide - (own_second + returned) * atom_mask[:, None, :]
    rho_now = sums[0:2]
    curv_now = sums[2:4]
    image_pre = sums[4:6]
    search_cross = sums[6:8]
    scaled_curv = sums[8:10]
    step_now = rho_now / curv_now
    step_size = spread_sets(step_now)
    dipoles = step_size * search
    residual = residual - step_size * image
    precond = pol_wide * residual
    precond_image = image - step_size * image_scaled
    rho_next = rho_now - 2.0 * step_now * curv_now + step_now * step_now * image_pre
    mixed = image_pre + search_cross
    precond_curv = curv_now - step_now * mixed + step_now * step_now * scaled_curv
    cross = 2.0 * curv_now - step_now * mixed
    ratio = rho_next / rho_now
    curv_next = precond_curv + ratio * cross + ratio * ratio * curv_now
    ratio_wide = spread_sets(ratio)
    search = precond + ratio_wide * search
    image = precond_image + ratio_wide * image
    step_size = spread_sets(rho_next / curv_next)
    dipoles = dipoles + step_size * search
    residual = residual - step_size * image
    return (dipoles[None, None], residual[None, None])


def solution(mesh):
    in_specs = (
        P("gx", "gy", None, None, None),
        P("gx", "gy", None, None),
        P("gx", "gy", None, None, None),
        P("gx", "gy", None),
        P("gx", "gy", None, None),
        P("gx", "gy"),
    )
    out_specs = (P("gx", "gy", None, None, None), P("gx", "gy", None, None, None))
    return jax.shard_map(
        per_device, mesh=mesh, in_specs=in_specs, out_specs=out_specs, check_vma=False
    )
```

```python
import jax
import jax.numpy as jnp
from jax import lax
from jax.sharding import PartitionSpec as P

ITERS = 2


thole_factor = 0.39
column_width = 8.0
slot_shift_x = (0.0, 0.0, 1.0, 1.0, 1.0)
slot_shift_y = (0.0, 1.0, -1.0, 0.0, 1.0)


def padded_2(cells, sides, width):
    for axis, dim in sides:
        count = lax.axis_size(axis)
        head = lax.slice_in_dim(cells, 0, width, axis=dim)
        tail = lax.slice_in_dim(cells, cells.shape[dim] - width, cells.shape[dim], axis=dim)
        cells = jnp.concatenate(
            [
                lax.ppermute(tail, axis, [(i, (i + 1) % count) for i in range(count)]),
                cells,
                lax.ppermute(head, axis, [((i + 1) % count, i) for i in range(count)]),
            ],
            axis=dim,
        )
    return cells


def from_behind(value, axis, steps):
    count = lax.axis_size(axis)
    pairs = [(source, (source + steps) % count) for source in range(count)]
    return lax.ppermute(value, axis, pairs)


def tensor_apply(coef_three, coef_five, deltas, moment, axis_sum):
    if axis_sum == 2:
        moments = [moment[:, member, None, :] for member in range(3)]
    else:
        moments = [moment[:, member, :, None] for member in range(3)]
    project = deltas[0] * moments[0] + deltas[1] * moments[1] + deltas[2] * moments[2]
    scaled = coef_five * project
    return jnp.stack(
        [
            jnp.sum(scaled * deltas[member] - coef_three * moments[member], axis=axis_sum)
            for member in range(3)
        ],
        axis=1,
    )


def pair_fields(geom_i, geom_j, dip_i, dip_j, slot_ids, same_block, two_way=True):
    chosen = (slot_ids[:, None] == jnp.arange(5, dtype=jnp.int32)[None, :]).astype(jnp.float32)
    offset_x = column_width * jnp.sum(
        chosen * jnp.array(slot_shift_x, jnp.float32)[None, :], axis=1
    )
    offset_y = column_width * jnp.sum(
        chosen * jnp.array(slot_shift_y, jnp.float32)[None, :], axis=1
    )
    delta_x = geom_j[:, 0, None, :] + offset_x[:, None, None] - geom_i[:, 0, :, None]
    delta_y = geom_j[:, 1, None, :] + offset_y[:, None, None] - geom_i[:, 1, :, None]
    delta_z = geom_j[:, 2, None, :] - geom_i[:, 2, :, None]
    dist_sq = delta_x * delta_x + delta_y * delta_y + delta_z * delta_z
    atom_width = geom_i.shape[2]
    same_atom = jnp.arange(atom_width)[:, None] == jnp.arange(atom_width)[None, :]
    diagonal = same_atom[None, :, :] & same_block[:, None, None]
    dist_sq = jnp.where(diagonal, 1.0, dist_sq)
    inv_dist = lax.rsqrt(dist_sq)
    inv_cube = inv_dist * inv_dist * inv_dist
    root_pol = jnp.sqrt(geom_i[:, 3, :, None] * geom_j[:, 3, None, :])
    damping = thole_factor * dist_sq * jnp.sqrt(dist_sq) / root_pol
    lambda_three = -jnp.expm1(-damping)
    lambda_five = lambda_three - damping * jnp.exp(-damping)
    keep_pair = jnp.where(diagonal, 0.0, 1.0)
    coef_three = keep_pair * lambda_three * inv_cube
    coef_five = keep_pair * 3.0 * lambda_five * inv_cube * inv_dist * inv_dist
    deltas = (delta_x, delta_y, delta_z)
    forward = jnp.concatenate(
        [
            tensor_apply(coef_three, coef_five, deltas, dip_j[:, 0:3], 2),
            tensor_apply(coef_three, coef_five, deltas, dip_j[:, 3:6], 2),
        ],
        axis=1,
    )
    if not two_way:
        return (forward, None)
    backward = jnp.concatenate(
        [
            tensor_apply(coef_three, coef_five, deltas, dip_i[:, 0:3], 1),
            tensor_apply(coef_three, coef_five, deltas, dip_i[:, 3:6], 1),
        ],
        axis=1,
    )
    return (forward, backward)


def pair_presence(entries, pair_total, blocks):
    live = jnp.arange(entries.shape[1], dtype=jnp.int32) < pair_total
    own_block, slot_ids, other_block = entries[0], entries[1], entries[2]
    shift = other_block - own_block + 1
    hit = (
        live[:, None, None, None]
        & (slot_ids[:, None, None, None] == jnp.arange(5, dtype=jnp.int32)[None, :, None, None])
        & (shift[:, None, None, None] == jnp.arange(3, dtype=jnp.int32)[None, None, :, None])
        & (own_block[:, None, None, None] == jnp.arange(blocks, dtype=jnp.int32)[None, None, None, :])
    )
    return jnp.sum(hit.astype(jnp.float32), axis=0)


def shifted_batch(own, other, blocks):
    first = jnp.concatenate([own[1:blocks], own, own[0 : blocks - 1]], axis=0)
    second = jnp.concatenate([other[0 : blocks - 1], other, other[1:blocks]], axis=0)
    return first, second


def gated(values, present):
    return jnp.where(present[:, None, None] > 0, values, 0.0)


def accumulate(geom_stack, dip_stack, presence):
    blocks = geom_stack.shape[1]
    geom_own = geom_stack[0]
    dip_own = dip_stack[0]
    same, _ = pair_fields(
        geom_own,
        geom_own,
        dip_own,
        dip_own,
        jnp.zeros((blocks,), jnp.int32),
        jnp.ones((blocks,), bool),
        two_way=False,
    )
    own_total = gated(same, presence[0, 1])
    count = blocks - 1
    forward, backward = pair_fields(
        geom_own[0:count],
        geom_own[1:blocks],
        dip_own[0:count],
        dip_own[1:blocks],
        jnp.zeros((count,), jnp.int32),
        jnp.zeros((count,), bool),
    )
    near = presence[0, 2, 0:count]
    zero_block = jnp.zeros_like(own_total[0:1])
    own_total = own_total + jnp.concatenate([gated(forward, near), zero_block], axis=0)
    own_total = own_total + jnp.concatenate([zero_block, gated(backward, near)], axis=0)
    own_i, _ = shifted_batch(geom_own, geom_own, blocks)
    dip_i, _ = shifted_batch(dip_own, dip_own, blocks)
    width = 3 * blocks - 2

    def one_slot(slot_index, carry):
        own_acc, other_acc = carry
        geom_j = lax.dynamic_index_in_dim(geom_stack, slot_index, 0, keepdims=False)
        dip_j = lax.dynamic_index_in_dim(dip_stack, slot_index, 0, keepdims=False)
        _, geom_j = shifted_batch(geom_j, geom_j, blocks)
        _, dip_j = shifted_batch(dip_j, dip_j, blocks)
        listed = lax.dynamic_index_in_dim(presence, slot_index, 0, keepdims=False)
        present = jnp.concatenate([listed[0, 1:blocks], listed[1], listed[2, 0:count]])
        forward, backward = pair_fields(
            own_i,
            geom_j,
            dip_i,
            dip_j,
            jnp.full((width,), slot_index, jnp.int32),
            jnp.zeros((width,), bool),
        )
        forward = gated(forward, present)
        backward = gated(backward, present)
        own_acc = (
            own_acc
            + jnp.concatenate([zero_block, forward[0:count]], axis=0)
            + forward[count : count + blocks]
            + jnp.concatenate([forward[count + blocks : width], zero_block], axis=0)
        )
        other_sum = (
            jnp.concatenate([backward[0:count], zero_block], axis=0)
            + backward[count : count + blocks]
            + jnp.concatenate([zero_block, backward[count + blocks : width]], axis=0)
        )
        other_acc = lax.dynamic_update_index_in_dim(other_acc, other_sum, slot_index - 1, 0)
        return own_acc, other_acc

    other_acc = jnp.zeros((4,) + own_total.shape, jnp.float32)
    carry = lax.fori_loop(2, 5, one_slot, (own_total, other_acc))
    return one_slot(1, carry)


def neighbours(block_data):
    column = padded_2(block_data[None, None], (("gy", 1),), 1)
    across = from_behind(column, "gx", -1)
    return jnp.concatenate([block_data[None], column[0, 2:3], across[0]], axis=0)


def send_back(partials):
    received = from_behind(partials[None, 1:4], "gx", 1)
    paired = jnp.stack([received[0, 0], received[0, 2] + partials[0]], axis=0)[None]
    column = padded_2(paired, (("gy", 1),), 1)
    return column[0, 0] + column[0, 3] + received[0, 1]


def set_sums(first_vec, second_vec):
    product = (first_vec * second_vec).reshape(first_vec.shape[0], 2, 3, first_vec.shape[2])
    return jnp.sum(product, axis=(0, 2, 3))


def spread_sets(values):
    return jnp.repeat(values, 3)[None, :, None]


def butterfly_sum(values, axis, first=1, last=None):
    count = lax.axis_size(axis)
    bound = count if last is None else min(last, count)
    stride = first
    while stride < bound:
        partner = lax.ppermute(values, axis, [(i, i ^ stride) for i in range(count)])
        values = values + partner
        stride *= 2
    return values


def field_dot(values, own_total, other_acc):
    total = set_sums(values[0], own_total)
    for slot_index in range(other_acc.shape[0]):
        total = total + set_sums(values[slot_index + 1], other_acc[slot_index])
    return total


def global_sums(local_values):
    return butterfly_sum(butterfly_sum(local_values, "gx"), "gy")


def per_device(positions, polarity, direct_field, atom_count, pair_list, pair_count):
    blocks = positions.shape[2]
    atom_width = positions.shape[4]
    atom_mask = (
        jnp.arange(atom_width, dtype=jnp.int32)[None, :] < atom_count[0, 0][:, None]
    ).astype(jnp.float32)
    pol_wide = polarity[0, 0][:, None, :]
    geometry = jnp.concatenate([positions[0, 0], pol_wide], axis=1)
    entries = pair_list[0, 0]
    pair_total = pair_count[0, 0]
    presence = pair_presence(entries, pair_total, blocks)

    def mutual_field(geom_stack, dip_stack):
        own_total, other_acc = accumulate(geom_stack, dip_stack, presence)
        return (own_total + send_back(other_acc)) * atom_mask[:, None, :]

    residual = direct_field[0, 0] * atom_mask[:, None, :]
    search = pol_wide * residual
    stacked = neighbours(jnp.concatenate([geometry, search], axis=1))
    geom_stack = stacked[:, :, 0:4]
    dip_stack = stacked[:, :, 4:10]
    image = search / pol_wide - mutual_field(geom_stack, dip_stack)
    scaled = pol_wide * image
    scaled_dip = neighbours(scaled)
    own_second, other_second = accumulate(geom_stack, scaled_dip, presence)
    search_field = field_dot(dip_stack, own_second, other_second)
    scaled_field = field_dot(scaled_dip, own_second, other_second)
    sums = butterfly_sum(
        jnp.concatenate(
            [
                set_sums(residual, search),
                set_sums(search, image),
                set_sums(image, scaled),
                set_sums(search, scaled / pol_wide) - search_field,
                set_sums(scaled, scaled / pol_wide) - scaled_field,
            ]
        ),
        "gx",
    )
    sums, other_second = lax.optimization_barrier((sums, other_second))
    received = from_behind(other_second[None, 1:4], "gx", 1)
    sums = butterfly_sum(sums, "gy", last=4)
    sums, received = lax.optimization_barrier((sums, received))
    paired = jnp.stack([received[0, 0], received[0, 2] + other_second[0]], axis=0)[None]
    column = padded_2(paired, (("gy", 1),), 1)
    sums = butterfly_sum(sums, "gy", first=4)
    returned = column[0, 0] + column[0, 3] + received[0, 1]
    image_scaled = scaled / pol_wide - (own_second + returned) * atom_mask[:, None, :]
    rho_now = sums[0:2]
    curv_now = sums[2:4]
    image_pre = sums[4:6]
    search_cross = sums[6:8]
    scaled_curv = sums[8:10]
    step_now = rho_now / curv_now
    step_size = spread_sets(step_now)
    dipoles = step_size * search
    residual = residual - step_size * image
    precond = pol_wide * residual
    precond_image = image - step_size * image_scaled
    rho_next = rho_now - 2.0 * step_now * curv_now + step_now * step_now * image_pre
    mixed = image_pre + search_cross
    precond_curv = curv_now - step_now * mixed + step_now * step_now * scaled_curv
    cross = 2.0 * curv_now - step_now * mixed
    ratio = rho_next / rho_now
    curv_next = precond_curv + ratio * cross + ratio * ratio * curv_now
    ratio_wide = spread_sets(ratio)
    search = precond + ratio_wide * search
    image = precond_image + ratio_wide * image
    step_size = spread_sets(rho_next / curv_next)
    dipoles = dipoles + step_size * search
    residual = residual - step_size * image
    return (dipoles[None, None], residual[None, None])


def solution(mesh):
    in_specs = (
        P("gx", "gy", None, None, None),
        P("gx", "gy", None, None),
        P("gx", "gy", None, None, None),
        P("gx", "gy", None),
        P("gx", "gy", None, None),
        P("gx", "gy"),
    )
    out_specs = (P("gx", "gy", None, None, None), P("gx", "gy", None, None, None))
    return jax.shard_map(
        per_device, mesh=mesh, in_specs=in_specs, out_specs=out_specs, check_vma=False
    )
```
